256 devices in a mesh: slab: 32 (over z, x), coil: 8 (over y, core).
Axes of the slice: x: 4, y: 4, z: 8, core: 2. Of those that a mesh axis runs over, the one named last changes fastest.
Arguments:
- noisy: float32 [2, 64, 256, 128], P(None, 'slab', 'coil'), may hold values from -6 to 6
- step_index: int32 [], replicated, may hold values from 200 to 599
- w_in: bfloat16 [3, 3, 3, 32, 2], replicated, may hold values from -0.875 to 0.875
- w_mid: bfloat16 [3, 3, 3, 32, 32], replicated, may hold values from -0.21875 to 0.21875
- w_out: bfloat16 [3, 3, 3, 2, 32], replicated, may hold values from -0.21875 to 0.21875
- time_weight: float32 [32, 32], replicated, may hold values from -1 to 1
- sens: float32 [16, 2, 64, 256, 128], P('coil', None, 'slab')
- kdata: float32 [16, 2, 64, 256, 128], P('coil', None, None, 'slab'), may hold values from -4 to 4
- mask: int32 [64, 256], P(None, 'slab'), may hold values from 0 to 1, as said below
Outputs:
- recon: float32 [2, 64, 256, 128], P(None, 'slab', 'coil')
- next_sample: float32 [2, 64, 256, 128], P(None, 'slab', 'coil')
The draws below stay inside these ranges and needn't reach their ends.
Inputs may be any that keep to these rules, and one draw needn't show every extreme that they name: mask[kz, ky] is 1 wherever min(kz, 64 - kz) < max(1, 4) and min(ky, 256 - ky) < max(1, 8); every other entry is 1 with chance one in three.
All inputs are finite; a program needn't handle non-finite values.
Results may differ from the reference program's by a relative error of at most 0.0023.
Values may be sent and summed in bfloat16 or wider, within the bound.
No kernel may reach another device: no remote copies, remote signals or barrier semaphores. Data moves between devices by JAX's collectives and lax.ppermute only.
A program may use at most 64 MiB of HBM per device.

```python
import math
import jax
import jax.numpy as jnp
from jax import lax

NY = 256
NX = 128
CH = 32
ITERS = 2
STEPS = 1000
STRIDE = 20
NZ = 64
COILS = 16


def draw_sens(key, part):
    shape = (COILS, 2, NZ, NY, NX)
    white_key = jax.random.fold_in(key, 11)
    depth = jnp.arange(NZ, dtype=jnp.float32) / max(NZ - 1, 1)
    depth_pos = jnp.arange(NZ, dtype=jnp.float32) / NZ
    row_pos = jnp.arange(NY, dtype=jnp.float32) / NY
    readout_ramp = 3.0 * jnp.arange(NX, dtype=jnp.float32) / max(NX - 1, 1)
    freq_depth = jax.random.uniform(jax.random.fold_in(key, 21), (COILS, 2, 3), jnp.float32, 0.0, 1.5)
    freq_rows = jax.random.uniform(jax.random.fold_in(key, 22), (COILS, 2, 3), jnp.float32, 0.0, 2.0)
    phases = jax.random.uniform(jax.random.fold_in(key, 23), (COILS, 2, 3), jnp.float32, -math.pi, math.pi)
    coefs = jax.random.normal(jax.random.fold_in(key, 24), (COILS, 2, 3), jnp.float32)
    amplitude = jax.random.uniform(jax.random.fold_in(key, 25), (COILS,), jnp.float32, 0.0, 1.0)
    profile = jnp.zeros((COILS, 2, NZ, NY), jnp.float32)
    for term_index in range(3):
        angle = 2.0 * math.pi * (freq_depth[:, :, term_index, None, None] * depth_pos[:, None] + freq_rows[:, :, term_index, None, None] * row_pos[None, :]) + phases[:, :, term_index, None, None]
        profile = profile + coefs[:, :, term_index, None, None] * jnp.cos(angle)
    profile = profile * math.sqrt(2.0 / 3.0)
    smooth = amplitude[:, None, None, None, None] * profile[..., None] * readout_ramp[None, None, None, None, :]
    ramp = 0.6 + 0.6 * depth
    values = jax.random.normal(white_key, shape, jnp.float32)
    return (values + smooth) * ramp[None, None, :, None, None] / math.sqrt(2.0 * COILS)


def draw_mask(key, part):
    picks = jax.random.randint(key, (NZ, NY), 0, 3, dtype=jnp.int32) == 0
    depth_index = jnp.arange(NZ, dtype=jnp.int32)
    row_index = jnp.arange(NY, dtype=jnp.int32)
    depth_near = jnp.minimum(depth_index, NZ - depth_index) < max(1, NZ // 16)
    row_near = jnp.minimum(row_index, NY - row_index) < max(1, NY // 32)
    centre = depth_near[:, None] & row_near[None, :]
    return (picks | centre).astype(jnp.int32)


def block_levels(rng, shape, shards, low, top_value):
    level = 1.0
    for position, shards_of in shards:
        heights = jax.random.uniform(jax.random.fold_in(jax.random.fold_in(rng, 6), position), (shards_of,), jnp.float32, low / len(shards), top_value / len(shards))
        level = level * jnp.repeat(jnp.exp(heights), shape[position] // shards_of).reshape((-1,) + (1,) * (len(shape) - 1 - position))
    return level


def bell_draw(stream_key, extent, deviation, bound, cuts=(), held_as=jnp.bfloat16):
    array = deviation * jax.random.normal(stream_key, extent, jnp.float32)
    if cuts:
        array = array * block_levels(stream_key, extent, cuts, -0.22, 0.18)
    return jnp.clip(array, -bound, bound).astype(held_as)


def setup_inputs(seed: int = 0) -> dict:
    key_list = jax.random.split(jax.random.key(seed), 10)
    noisy = bell_draw(key_list[0], (2, NZ, NY, NX), 1.0, 6.0, ((1, 32), (2, 8)), jnp.float32)
    step_index = jax.random.randint(key_list[1], (), 200, 600).astype(jnp.int32)
    w_in = bell_draw(key_list[2], (3, 3, 3, CH, 2), 54 ** -0.5, 0.875)
    w_mid = bell_draw(key_list[3], (3, 3, 3, CH, CH), (27 * CH) ** -0.5, 0.21875)
    w_out = bell_draw(key_list[4], (3, 3, 3, 2, CH), (27 * CH) ** -0.5, 0.21875)
    time_weight = bell_draw(key_list[5], (CH, CH), CH ** -0.5, 1.0, (), jnp.float32)
    sens = draw_sens(jax.random.fold_in(key_list[9], 71), 0)
    kdata = bell_draw(key_list[7], (COILS, 2, NZ, NY, NX), 0.5, 4.0, ((0, 8), (3, 32)), jnp.float32)
    mask = draw_mask(jax.random.fold_in(key_list[9], 71), 0)
    return {"noisy": noisy, "step_index": step_index, "w_in": w_in, "w_mid": w_mid, "w_out": w_out, "time_weight": time_weight, "sens": sens, "kdata": kdata, "mask": mask}


REG_WEIGHT = 0.5

def plan_level(step_value):
    angle = (step_value / STEPS + 0.008) / 1.008 * (math.pi / 2)
    return jnp.cos(angle) ** 2

def time_bias(step_value, time_weight):
    half = time_weight.shape[0] // 2
    freqs = jnp.exp(-math.log(10000.0) * jnp.arange(half, dtype=jnp.float32) / half)
    phase = step_value * freqs
    embed = jnp.concatenate([jnp.sin(phase), jnp.cos(phase)])
    return jnp.dot(embed, time_weight, precision=lax.Precision.HIGHEST)

def conv_ref(inputs, weights):
    kernel = jnp.transpose(weights.astype(jnp.float32), (3, 4, 0, 1, 2))
    result = lax.conv_general_dilated(inputs.astype(jnp.float32)[None], kernel, (1, 1, 1), ((1, 1), (1, 1), (1, 1)), dimension_numbers=('NCDHW', 'OIDHW', 'NCDHW'), precision=lax.Precision.HIGHEST)
    return result[0]

def reference(noisy, step_index, w_in, w_mid, w_out, time_weight, sens, kdata, mask):
    step_value = step_index.astype(jnp.float32)
    signal_level = plan_level(step_value)
    prior_level = plan_level(step_value - STRIDE)
    bias = time_bias(step_value, time_weight)
    hidden = jax.nn.silu(conv_ref(noisy.astype(jnp.bfloat16), w_in) + bias[:, None, None, None]).astype(jnp.bfloat16)
    mixed = (hidden.astype(jnp.float32) + jax.nn.silu(conv_ref(hidden, w_mid))).astype(jnp.bfloat16)
    noise_pred = conv_ref(mixed, w_out)
    estimate = (noisy - jnp.sqrt(1.0 - signal_level) * noise_pred) / jnp.sqrt(signal_level)
    weight = mask.astype(jnp.float32)[:, :, None]

    def coil_term(image, with_data):
        image_c = lax.complex(image[0], image[1])

        def per_coil(total, pieces):
            sens_c, data_c = pieces
            profile = lax.complex(sens_c[0], sens_c[1])
            spectrum = jnp.fft.fftn(profile * image_c, norm='ortho')
            if with_data:
                spectrum = weight * (lax.complex(data_c[0], data_c[1]) - spectrum)
            else:
                spectrum = weight * spectrum
            back = jnp.fft.ifftn(spectrum, norm='ortho')
            return (total + jnp.conj(profile) * back, None)
        total, _ = lax.scan(per_coil, jnp.zeros_like(image_c), (sens, kdata))
        return jnp.stack([jnp.real(total), jnp.imag(total)])
    solution = estimate
    residual = coil_term(estimate, True)
    direction = residual
    norm_now = jnp.sum(residual * residual)
    for iteration in range(ITERS):
        image = coil_term(direction, False) + REG_WEIGHT * direction
        step_size = norm_now / jnp.sum(direction * image)
        solution = solution + step_size * direction
        if iteration + 1 < ITERS:
            residual = residual - step_size * image
            norm_next = jnp.sum(residual * residual)
            direction = residual + norm_next / norm_now * direction
            norm_now = norm_next
    next_sample = jnp.sqrt(prior_level) * solution + jnp.sqrt(1.0 - prior_level) * noise_pred
    return (solution, next_sample)
```

```python
import math

import jax
import jax.numpy as jnp
from jax import lax
from jax.sharding import PartitionSpec as P

ITERS = 2
STEPS = 1000
STRIDE = 20


REG_WEIGHT = 0.5
HIGHEST_PRECISION = lax.Precision.HIGHEST


def extended(cells, sides, width):
    for axis, dim in sides:
        count = lax.axis_size(axis)
        ends = count - 1
        head = lax.slice_in_dim(cells, 0, width, axis=dim)
        tail = lax.slice_in_dim(cells, cells.shape[dim] - width, cells.shape[dim], axis=dim)
        cells = jnp.concatenate(
            [
                lax.ppermute(tail, axis, [(i, (i + 1) % count) for i in range(ends)]),
                cells,
                lax.ppermute(head, axis, [((i + 1) % count, i) for i in range(ends)]),
            ],
            axis=dim,
        )
    return cells


def plan_level(step_value):
    angle = (step_value / STEPS + 0.008) / 1.008 * (math.pi / 2)
    return jnp.cos(angle) ** 2


def time_bias(step_value, time_weight):
    half = time_weight.shape[0] // 2
    freqs = jnp.exp(-math.log(10000.0) * jnp.arange(half, dtype=jnp.float32) / half)
    phase = step_value * freqs
    embed = jnp.concatenate([jnp.sin(phase), jnp.cos(phase)])
    return jnp.dot(embed, time_weight, precision=HIGHEST_PRECISION)


def conv_layer(inputs, weights):
    depth, rows, width = (inputs.shape[1], inputs.shape[2], inputs.shape[3])
    padded = extended(inputs, (("slab", 1), ("coil", 2)), 1)
    total = jnp.zeros((weights.shape[3], depth, rows, width), jnp.float32)
    for depth_shift in range(3):
        for row_shift in range(3):
            window = padded[:, depth_shift : depth_shift + depth, row_shift : row_shift + rows, :]
            taps = jnp.einsum(
                "aoc,czyx->aozyx",
                weights[depth_shift, row_shift],
                window,
                preferred_element_type=jnp.float32,
            )
            shifted = jnp.pad(taps, ((0, 0), (0, 0), (0, 0), (0, 0), (1, 1)))
            total = (
                total
                + shifted[0, ..., 0:width]
                + shifted[1, ..., 1 : width + 1]
                + shifted[2, ..., 2 : width + 2]
            )
    return total


def dft_blocks(length, inverse):
    index = jnp.arange(length, dtype=jnp.int32)
    product = index[:, None] * index[None, :] % length
    theta = product.astype(jnp.float32) * (2.0 * math.pi / length)
    cosine = jnp.cos(theta) / math.sqrt(length)
    sine = jnp.sin(theta) / math.sqrt(length)
    if inverse:
        sine = -sine
    upper = jnp.stack([cosine, sine], axis=1)
    lower = jnp.stack([-sine, cosine], axis=1)
    return jnp.stack([upper, lower], axis=0)


def along_last(data, blocks):
    return jnp.einsum("pkqn,cqzyn->cpzyk", blocks, data, precision=HIGHEST_PRECISION)


def along_rows(data, blocks):
    return jnp.einsum("pkqn,cqzny->cpzky", blocks, data, precision=HIGHEST_PRECISION)


def along_depth(data, blocks):
    return jnp.einsum("pkqn,cqnyx->cpkyx", blocks, data, precision=HIGHEST_PRECISION)


def times_sens(sens, image):
    real_part = sens[:, 0] * image[0] - sens[:, 1] * image[1]
    imag_part = sens[:, 0] * image[1] + sens[:, 1] * image[0]
    return jnp.stack([real_part, imag_part], axis=1)


def times_conj(sens, images):
    real_part = jnp.sum(sens[:, 0] * images[:, 0] + sens[:, 1] * images[:, 1], axis=0)
    imag_part = jnp.sum(sens[:, 0] * images[:, 1] - sens[:, 1] * images[:, 0], axis=0)
    return jnp.stack([real_part, imag_part])


def coil_term(image_full, sens, kdata_x, weight, blocks, with_data):
    forward_y, forward_z, inverse_y, inverse_z = blocks
    coil_images = times_sens(sens, image_full)
    spectrum = along_rows(coil_images, forward_y)
    pencils = lax.all_to_all(spectrum, "slab", split_axis=3, concat_axis=2, tiled=True)
    kspace = along_depth(pencils, forward_z)
    if with_data:
        kspace = weight * (kdata_x - kspace)
    else:
        kspace = weight * kspace
    back = along_depth(kspace, inverse_z)
    slabs = lax.all_to_all(back, "slab", split_axis=2, concat_axis=3, tiled=True)
    images = along_rows(slabs, inverse_y)
    return times_conj(sens, images)


def combine_coils(partial_value):
    count = lax.axis_size("coil")
    pieces = lax.all_to_all(partial_value, "coil", split_axis=2, concat_axis=0, tiled=True)
    pieces = pieces.reshape((count, partial_value.shape[0]) + pieces.shape[1:])
    return jnp.sum(pieces, axis=0)


def gather_rows(value):
    return lax.all_gather(value, "coil", axis=2, tiled=True)


def global_sums(values):
    axes = ("slab", "coil")
    count = lax.axis_size("slab") * lax.axis_size("coil")
    spread = jnp.broadcast_to(values[None], (count,) + values.shape)
    return jnp.sum(lax.all_to_all(spread, axes, split_axis=0, concat_axis=0, tiled=True), axis=0)


def body(noisy, step_index, w_in, w_mid, w_out, time_weight, sens, kdata, mask):
    step_value = step_index.astype(jnp.float32)
    signal_level = plan_level(step_value)
    prior_level = plan_level(step_value - STRIDE)
    bias = time_bias(step_value, time_weight)
    hidden = jax.nn.silu(
        conv_layer(noisy.astype(jnp.bfloat16), w_in) + bias[:, None, None, None]
    ).astype(jnp.bfloat16)
    mixed = (hidden.astype(jnp.float32) + jax.nn.silu(conv_layer(hidden, w_mid))).astype(
        jnp.bfloat16
    )
    noise_pred = conv_layer(mixed, w_out)
    estimate = (noisy - jnp.sqrt(1.0 - signal_level) * noise_pred) / jnp.sqrt(signal_level)
    depth_full = kdata.shape[2]
    rows_full = sens.shape[3]
    width = sens.shape[4]
    blocks = (
        dft_blocks(rows_full, False),
        dft_blocks(depth_full, False),
        dft_blocks(rows_full, True),
        dft_blocks(depth_full, True),
    )
    kdata_x = along_last(kdata, dft_blocks(width, True))
    weight = mask.astype(jnp.float32)[None, None, :, :, None]

    def operator(image, with_data):
        return combine_coils(
            coil_term(gather_rows(image), sens, kdata_x, weight, blocks, with_data)
        )

    solution = estimate
    residual = operator(estimate, True)
    direction = residual
    norm_now = None
    for iteration in range(ITERS):
        final_turn = iteration + 1 == ITERS
        image = operator(direction, False) + REG_WEIGHT * direction
        if norm_now is None:
            sums = global_sums(jnp.stack([jnp.sum(residual * residual), jnp.sum(direction * image)]))
            norm_now, curvature = sums[0], sums[1]
        else:
            curvature = global_sums(jnp.stack([jnp.sum(direction * image)]))[0]
        step_size = norm_now / curvature
        solution = solution + step_size * direction
        if not final_turn:
            residual = residual - step_size * image
            norm_next = global_sums(jnp.stack([jnp.sum(residual * residual)]))[0]
            direction = residual + norm_next / norm_now * direction
            norm_now = norm_next
    recon = solution
    next_sample = jnp.sqrt(prior_level) * recon + jnp.sqrt(1.0 - prior_level) * noise_pred
    return (recon, next_sample)


def solution(mesh):
    return jax.shard_map(
        body,
        mesh=mesh,
        in_specs=(
            P(None, "slab", "coil", None),
            P(),
            P(),
            P(),
            P(),
            P(),
            P("coil", None, "slab", None, None),
            P("coil", None, None, "slab", None),
            P(None, "slab"),
        ),
        out_specs=(P(None, "slab", "coil", None), P(None, "slab", "coil", None)),
        check_vma=False,
    )
```

```python
import math

import jax
import jax.numpy as jnp
from jax import lax
from jax.sharding import PartitionSpec as P

ITERS = 2
STEPS = 1000
STRIDE = 20


REG_WEIGHT = 0.5
HIGHEST_PRECISION = lax.Precision.HIGHEST


def extended(cells, sides, width):
    for axis, dim in sides:
        count = lax.axis_size(axis)
        ends = count - 1
        head = lax.slice_in_dim(cells, 0, width, axis=dim)
        tail = lax.slice_in_dim(cells, cells.shape[dim] - width, cells.shape[dim], axis=dim)
        cells = jnp.concatenate(
            [
                lax.ppermute(tail, axis, [(i, (i + 1) % count) for i in range(ends)]),
                cells,
                lax.ppermute(head, axis, [((i + 1) % count, i) for i in range(ends)]),
            ],
            axis=dim,
        )
    return cells


def plan_level(step_value):
    angle = (step_value / STEPS + 0.008) / 1.008 * (math.pi / 2)
    return jnp.cos(angle) ** 2


def time_bias(step_value, time_weight):
    half = time_weight.shape[0] // 2
    freqs = jnp.exp(-math.log(10000.0) * jnp.arange(half, dtype=jnp.float32) / half)
    phase = step_value * freqs
    embed = jnp.concatenate([jnp.sin(phase), jnp.cos(phase)])
    return jnp.dot(embed, time_weight, precision=HIGHEST_PRECISION)


def conv_layer(inputs, weights):
    depth, rows, width = (inputs.shape[1], inputs.shape[2], inputs.shape[3])
    padded = extended(inputs, (("slab", 1), ("coil", 2)), 1)
    total = jnp.zeros((weights.shape[3], depth, rows, width), jnp.float32)
    for depth_shift in range(3):
        for row_shift in range(3):
            window = padded[:, depth_shift : depth_shift + depth, row_shift : row_shift + rows, :]
            taps = jnp.einsum(
                "aoc,czyx->aozyx",
                weights[depth_shift, row_shift],
                window,
                preferred_element_type=jnp.float32,
            )
            shifted = jnp.pad(taps, ((0, 0), (0, 0), (0, 0), (0, 0), (1, 1)))
            total = (
                total
                + shifted[0, ..., 0:width]
                + shifted[1, ..., 1 : width + 1]
                + shifted[2, ..., 2 : width + 2]
            )
    return total


def dft_blocks(length, inverse):
    index = jnp.arange(length, dtype=jnp.int32)
    product = index[:, None] * index[None, :] % length
    theta = product.astype(jnp.float32) * (2.0 * math.pi / length)
    cosine = jnp.cos(theta) / math.sqrt(length)
    sine = jnp.sin(theta) / math.sqrt(length)
    if inverse:
        sine = -sine
    upper = jnp.stack([cosine, sine], axis=1)
    lower = jnp.stack([-sine, cosine], axis=1)
    return jnp.stack([upper, lower], axis=0)


def along_last(data, blocks):
    return jnp.einsum("pkqn,cqzyn->cpzyk", blocks, data, precision=HIGHEST_PRECISION)


def along_rows(data, blocks):
    return jnp.einsum("pkqn,cqzny->cpzky", blocks, data, precision=HIGHEST_PRECISION)


def along_depth(data, blocks):
    return jnp.einsum("pkqn,cqnyx->cpkyx", blocks, data, precision=HIGHEST_PRECISION)


def times_sens(sens, image):
    real_part = sens[:, 0] * image[0] - sens[:, 1] * image[1]
    imag_part = sens[:, 0] * image[1] + sens[:, 1] * image[0]
    return jnp.stack([real_part, imag_part], axis=1)


def times_conj(sens, images):
    real_part = jnp.sum(sens[:, 0] * images[:, 0] + sens[:, 1] * images[:, 1], axis=0)
    imag_part = jnp.sum(sens[:, 0] * images[:, 1] - sens[:, 1] * images[:, 0], axis=0)
    return jnp.stack([real_part, imag_part])


def coil_term(image_full, sens, kdata_x, weight, blocks, with_data):
    forward_y, forward_z, inverse_y, inverse_z = blocks
    coil_images = times_sens(sens, image_full)
    spectrum = along_rows(coil_images, forward_y)
    pencils = lax.all_to_all(
        spectrum.astype(jnp.bfloat16), "slab", split_axis=3, concat_axis=2, tiled=True
    ).astype(jnp.float32)
    kspace = along_depth(pencils, forward_z)
    if with_data:
        kspace = weight * (kdata_x - kspace)
    else:
        kspace = weight * kspace
    back = along_depth(kspace, inverse_z)
    slabs = lax.all_to_all(
        back.astype(jnp.bfloat16), "slab", split_axis=2, concat_axis=3, tiled=True
    ).astype(jnp.float32)
    images = along_rows(slabs, inverse_y)
    return times_conj(sens, images)


def combine_coils(partial_value):
    count = lax.axis_size("coil")
    pieces = lax.all_to_all(partial_value, "coil", split_axis=2, concat_axis=0, tiled=True)
    pieces = pieces.reshape((count, partial_value.shape[0]) + pieces.shape[1:])
    return jnp.sum(pieces, axis=0)


def gather_rows(value):
    return lax.all_gather(value, "coil", axis=2, tiled=True)


def global_sums(values):
    axes = ("slab", "coil")
    count = lax.axis_size("slab") * lax.axis_size("coil")
    spread = jnp.broadcast_to(values[None], (count,) + values.shape)
    return jnp.sum(lax.all_to_all(spread, axes, split_axis=0, concat_axis=0, tiled=True), axis=0)


def body(noisy, step_index, w_in, w_mid, w_out, time_weight, sens, kdata, mask):
    step_value = step_index.astype(jnp.float32)
    signal_level = plan_level(step_value)
    prior_level = plan_level(step_value - STRIDE)
    bias = time_bias(step_value, time_weight)
    hidden = jax.nn.silu(
        conv_layer(noisy.astype(jnp.bfloat16), w_in) + bias[:, None, None, None]
    ).astype(jnp.bfloat16)
    mixed = (hidden.astype(jnp.float32) + jax.nn.silu(conv_layer(hidden, w_mid))).astype(
        jnp.bfloat16
    )
    noise_pred = conv_layer(mixed, w_out)
    estimate = (noisy - jnp.sqrt(1.0 - signal_level) * noise_pred) / jnp.sqrt(signal_level)
    depth_full = kdata.shape[2]
    rows_full = sens.shape[3]
    width = sens.shape[4]
    blocks = (
        dft_blocks(rows_full, False),
        dft_blocks(depth_full, False),
        dft_blocks(rows_full, True),
        dft_blocks(depth_full, True),
    )
    kdata_x = along_last(kdata, dft_blocks(width, True))
    weight = mask.astype(jnp.float32)[None, None, :, :, None]

    def operator(image, with_data):
        return combine_coils(
            coil_term(gather_rows(image), sens, kdata_x, weight, blocks, with_data)
        )

    solution = estimate
    residual = operator(estimate, True)
    direction = residual
    norm_now = None
    for iteration in range(ITERS):
        final_turn = iteration + 1 == ITERS
        image = operator(direction, False) + REG_WEIGHT * direction
        if norm_now is None:
            sums = global_sums(jnp.stack([jnp.sum(residual * residual), jnp.sum(direction * image)]))
            norm_now, curvature = sums[0], sums[1]
        else:
            curvature = global_sums(jnp.stack([jnp.sum(direction * image)]))[0]
        step_size = norm_now / curvature
        solution = solution + step_size * direction
        if not final_turn:
            residual = residual - step_size * image
            norm_next = global_sums(jnp.stack([jnp.sum(residual * residual)]))[0]
            direction = residual + norm_next / norm_now * direction
            norm_now = norm_next
    recon = solution
    next_sample = jnp.sqrt(prior_level) * recon + jnp.sqrt(1.0 - prior_level) * noise_pred
    return (recon, next_sample)


def solution(mesh):
    return jax.shard_map(
        body,
        mesh=mesh,
        in_specs=(
            P(None, "slab", "coil", None),
            P(),
            P(),
            P(),
            P(),
            P(),
            P("coil", None, "slab", None, None),
            P("coil", None, None, "slab", None),
            P(None, "slab"),
        ),
        out_specs=(P(None, "slab", "coil", None), P(None, "slab", "coil", None)),
        check_vma=False,
    )
```

```python
import math

import jax
import jax.numpy as jnp
from jax import lax
from jax.sharding import PartitionSpec as P

ITERS = 2
STEPS = 1000
STRIDE = 20


REG_WEIGHT = 0.5
HIGHEST_PRECISION = lax.Precision.HIGHEST


def extended(cells, sides, width):
    for axis, dim in sides:
        count = lax.axis_size(axis)
        ends = count - 1
        head = lax.slice_in_dim(cells, 0, width, axis=dim)
        tail = lax.slice_in_dim(cells, cells.shape[dim] - width, cells.shape[dim], axis=dim)
        cells = jnp.concatenate(
            [
                lax.ppermute(tail, axis, [(i, (i + 1) % count) for i in range(ends)]),
                cells,
                lax.ppermute(head, axis, [((i + 1) % count, i) for i in range(ends)]),
            ],
            axis=dim,
        )
    return cells


def plan_level(step_value):
    angle = (step_value / STEPS + 0.008) / 1.008 * (math.pi / 2)
    return jnp.cos(angle) ** 2


def time_bias(step_value, time_weight):
    half = time_weight.shape[0] // 2
    freqs = jnp.exp(-math.log(10000.0) * jnp.arange(half, dtype=jnp.float32) / half)
    phase = step_value * freqs
    embed = jnp.concatenate([jnp.sin(phase), jnp.cos(phase)])
    return jnp.dot(embed, time_weight, precision=HIGHEST_PRECISION)


def conv_layer(inputs, weights):
    padded = extended(inputs, (("slab", 1), ("coil", 2)), 1)
    kernel = jnp.transpose(weights, (3, 4, 0, 1, 2))
    result = lax.conv_general_dilated(
        padded[None],
        kernel,
        (1, 1, 1),
        ((0, 0), (0, 0), (1, 1)),
        dimension_numbers=("NCDHW", "OIDHW", "NCDHW"),
        preferred_element_type=jnp.float32,
    )
    return result[0]


def dft_blocks(length, inverse):
    index = jnp.arange(length, dtype=jnp.int32)
    product = index[:, None] * index[None, :] % length
    theta = product.astype(jnp.float32) * (2.0 * math.pi / length)
    cosine = jnp.cos(theta) / math.sqrt(length)
    sine = jnp.sin(theta) / math.sqrt(length)
    if inverse:
        sine = -sine
    upper = jnp.stack([cosine, sine], axis=1)
    lower = jnp.stack([-sine, cosine], axis=1)
    return jnp.stack([upper, lower], axis=0)


def along_last(data, blocks):
    return jnp.einsum("pkqn,cqzyn->cpzyk", blocks, data, precision=HIGHEST_PRECISION)


def along_rows(data, blocks):
    return jnp.einsum("pkqn,cqzny->cpzky", blocks, data, precision=HIGHEST_PRECISION)


def along_depth(data, blocks):
    return jnp.einsum("pkqn,cqnyx->cpkyx", blocks, data, precision=HIGHEST_PRECISION)


def times_sens(sens, image):
    real_part = sens[:, 0] * image[0] - sens[:, 1] * image[1]
    imag_part = sens[:, 0] * image[1] + sens[:, 1] * image[0]
    return jnp.stack([real_part, imag_part], axis=1)


def times_conj(sens, images):
    real_part = jnp.sum(sens[:, 0] * images[:, 0] + sens[:, 1] * images[:, 1], axis=0)
    imag_part = jnp.sum(sens[:, 0] * images[:, 1] - sens[:, 1] * images[:, 0], axis=0)
    return jnp.stack([real_part, imag_part])


def coil_term(image_full, sens, kdata_x, weight, blocks, with_data):
    forward_y, forward_z, inverse_y, inverse_z = blocks
    coil_images = times_sens(sens, image_full)
    spectrum = along_rows(coil_images, forward_y)
    pencils = lax.all_to_all(
        spectrum.astype(jnp.bfloat16), "slab", split_axis=3, concat_axis=2, tiled=True
    ).astype(jnp.float32)
    kspace = along_depth(pencils, forward_z)
    if with_data:
        kspace = weight * (kdata_x - kspace)
    else:
        kspace = weight * kspace
    back = along_depth(kspace, inverse_z)
    slabs = lax.all_to_all(
        back.astype(jnp.bfloat16), "slab", split_axis=2, concat_axis=3, tiled=True
    ).astype(jnp.float32)
    images = along_rows(slabs, inverse_y)
    return times_conj(sens, images)


def combine_coils(partial_value):
    count = lax.axis_size("coil")
    pieces = lax.all_to_all(partial_value, "coil", split_axis=2, concat_axis=0, tiled=True)
    pieces = pieces.reshape((count, partial_value.shape[0]) + pieces.shape[1:])
    return jnp.sum(pieces, axis=0)


def gather_rows(value):
    return lax.all_gather(value, "coil", axis=2, tiled=True)


def global_sums(values):
    axes = ("slab", "coil")
    count = lax.axis_size("slab") * lax.axis_size("coil")
    spread = jnp.broadcast_to(values[None], (count,) + values.shape)
    return jnp.sum(lax.all_to_all(spread, axes, split_axis=0, concat_axis=0, tiled=True), axis=0)


def body(noisy, step_index, w_in, w_mid, w_out, time_weight, sens, kdata, mask):
    step_value = step_index.astype(jnp.float32)
    signal_level = plan_level(step_value)
    prior_level = plan_level(step_value - STRIDE)
    bias = time_bias(step_value, time_weight)
    hidden = jax.nn.silu(
        conv_layer(noisy.astype(jnp.bfloat16), w_in) + bias[:, None, None, None]
    ).astype(jnp.bfloat16)
    mixed = (hidden.astype(jnp.float32) + jax.nn.silu(conv_layer(hidden, w_mid))).astype(
        jnp.bfloat16
    )
    noise_pred = conv_layer(mixed, w_out)
    estimate = (noisy - jnp.sqrt(1.0 - signal_level) * noise_pred) / jnp.sqrt(signal_level)
    depth_full = kdata.shape[2]
    rows_full = sens.shape[3]
    width = sens.shape[4]
    blocks = (
        dft_blocks(rows_full, False),
        dft_blocks(depth_full, False),
        dft_blocks(rows_full, True),
        dft_blocks(depth_full, True),
    )
    kdata_x = along_last(kdata, dft_blocks(width, True))
    weight = mask.astype(jnp.float32)[None, None, :, :, None]

    def operator(image, with_data):
        return combine_coils(
            coil_term(gather_rows(image), sens, kdata_x, weight, blocks, with_data)
        )

    solution = estimate
    residual = operator(estimate, True)
    direction = residual
    norm_now = None
    for iteration in range(ITERS):
        final_turn = iteration + 1 == ITERS
        image = operator(direction, False) + REG_WEIGHT * direction
        if norm_now is None:
            sums = global_sums(jnp.stack([jnp.sum(residual * residual), jnp.sum(direction * image)]))
            norm_now, curvature = sums[0], sums[1]
        else:
            curvature = global_sums(jnp.stack([jnp.sum(direction * image)]))[0]
        step_size = norm_now / curvature
        solution = solution + step_size * direction
        if not final_turn:
            residual = residual - step_size * image
            norm_next = global_sums(jnp.stack([jnp.sum(residual * residual)]))[0]
            direction = residual + norm_next / norm_now * direction
            norm_now = norm_next
    recon = solution
    next_sample = jnp.sqrt(prior_level) * recon + jnp.sqrt(1.0 - prior_level) * noise_pred
    return (recon, next_sample)


def solution(mesh):
    return jax.shard_map(
        body,
        mesh=mesh,
        in_specs=(
            P(None, "slab", "coil", None),
            P(),
            P(),
            P(),
            P(),
            P(),
            P("coil", None, "slab", None, None),
            P("coil", None, None, "slab", None),
            P(None, "slab"),
        ),
        out_specs=(P(None, "slab", "coil", None), P(None, "slab", "coil", None)),
        check_vma=False,
    )
```

```python
import math

import jax
import jax.numpy as jnp
from jax import lax
from jax.sharding import PartitionSpec as P

ITERS = 2
STEPS = 1000
STRIDE = 20


REG_WEIGHT = 0.5
HIGHEST_PRECISION = lax.Precision.HIGHEST


def extended(cells, sides, width):
    for axis, dim in sides:
        count = lax.axis_size(axis)
        ends = count - 1
        head = lax.slice_in_dim(cells, 0, width, axis=dim)
        tail = lax.slice_in_dim(cells, cells.shape[dim] - width, cells.shape[dim], axis=dim)
        cells = jnp.concatenate(
            [
                lax.ppermute(tail, axis, [(i, (i + 1) % count) for i in range(ends)]),
                cells,
                lax.ppermute(head, axis, [((i + 1) % count, i) for i in range(ends)]),
            ],
            axis=dim,
        )
    return cells


def plan_level(step_value):
    angle = (step_value / STEPS + 0.008) / 1.008 * (math.pi / 2)
    return jnp.cos(angle) ** 2


def time_bias(step_value, time_weight):
    half = time_weight.shape[0] // 2
    freqs = jnp.exp(-math.log(10000.0) * jnp.arange(half, dtype=jnp.float32) / half)
    phase = step_value * freqs
    embed = jnp.concatenate([jnp.sin(phase), jnp.cos(phase)])
    return jnp.dot(embed, time_weight, precision=HIGHEST_PRECISION)


def conv_layer(inputs, weights):
    depth, rows, width = (inputs.shape[1], inputs.shape[2], inputs.shape[3])
    padded = extended(inputs, (("slab", 1), ("coil", 2)), 1)
    total = jnp.zeros((weights.shape[3], depth, rows, width), jnp.float32)
    for depth_shift in range(3):
        for row_shift in range(3):
            window = padded[:, depth_shift : depth_shift + depth, row_shift : row_shift + rows, :]
            taps = jnp.einsum(
                "aoc,czyx->aozyx",
                weights[depth_shift, row_shift],
                window,
                preferred_element_type=jnp.float32,
            )
            shifted = jnp.pad(taps, ((0, 0), (0, 0), (0, 0), (0, 0), (1, 1)))
            total = (
                total
                + shifted[0, ..., 0:width]
                + shifted[1, ..., 1 : width + 1]
                + shifted[2, ..., 2 : width + 2]
            )
    return total


def dft_blocks(length, inverse):
    index = jnp.arange(length, dtype=jnp.int32)
    product = index[:, None] * index[None, :] % length
    theta = product.astype(jnp.float32) * (2.0 * math.pi / length)
    cosine = jnp.cos(theta) / math.sqrt(length)
    sine = jnp.sin(theta) / math.sqrt(length)
    if inverse:
        sine = -sine
    upper = jnp.stack([cosine, sine], axis=1)
    lower = jnp.stack([-sine, cosine], axis=1)
    return jnp.stack([upper, lower], axis=0)


def along_last(data, blocks):
    return jnp.einsum("pkqn,cqzyn->cpzyk", blocks, data, precision=HIGHEST_PRECISION)


def along_rows(data, blocks):
    return jnp.einsum("pkqn,cqzny->cpzky", blocks, data, precision=HIGHEST_PRECISION)


def along_depth(data, blocks):
    return jnp.einsum("pkqn,cqnyx->cpkyx", blocks, data, precision=HIGHEST_PRECISION)


def times_sens(sens, image):
    real_part = sens[:, 0] * image[0] - sens[:, 1] * image[1]
    imag_part = sens[:, 0] * image[1] + sens[:, 1] * image[0]
    return jnp.stack([real_part, imag_part], axis=1)


def times_conj(sens, images):
    real_part = jnp.sum(sens[:, 0] * images[:, 0] + sens[:, 1] * images[:, 1], axis=0)
    imag_part = jnp.sum(sens[:, 0] * images[:, 1] - sens[:, 1] * images[:, 0], axis=0)
    return jnp.stack([real_part, imag_part])


def coil_term(image_full, sens, kdata_x, weight, blocks, with_data):
    forward_y, forward_z, inverse_y, inverse_z = blocks
    coil_images = times_sens(sens, image_full)
    spectrum = along_rows(coil_images, forward_y)
    pencils = lax.all_to_all(
        spectrum.astype(jnp.bfloat16), "slab", split_axis=3, concat_axis=2, tiled=True
    ).astype(jnp.float32)
    kspace = along_depth(pencils, forward_z)
    if with_data:
        kspace = weight * (kdata_x - kspace)
    else:
        kspace = weight * kspace
    back = along_depth(kspace, inverse_z)
    slabs = lax.all_to_all(
        back.astype(jnp.bfloat16), "slab", split_axis=2, concat_axis=3, tiled=True
    ).astype(jnp.float32)
    images = along_rows(slabs, inverse_y)
    return times_conj(sens, images)


def combine_coils(partial_value):
    count = lax.axis_size("coil")
    pieces = lax.all_to_all(partial_value, "coil", split_axis=2, concat_axis=0, tiled=True)
    pieces = pieces.reshape((count, partial_value.shape[0]) + pieces.shape[1:])
    return jnp.sum(pieces, axis=0)


def gather_rows(value):
    return lax.all_gather(value, "coil", axis=2, tiled=True)


def global_sums(values):
    axes = ("slab", "coil")
    count = lax.axis_size("slab") * lax.axis_size("coil")
    spread = jnp.broadcast_to(values[None], (count,) + values.shape)
    return jnp.sum(lax.all_to_all(spread, axes, split_axis=0, concat_axis=0, tiled=True), axis=0)


def body(noisy, step_index, w_in, w_mid, w_out, time_weight, sens, kdata, mask):
    step_value = step_index.astype(jnp.float32)
    signal_level = plan_level(step_value)
    prior_level = plan_level(step_value - STRIDE)
    bias = time_bias(step_value, time_weight)
    hidden = jax.nn.silu(
        conv_layer(noisy.astype(jnp.bfloat16), w_in) + bias[:, None, None, None]
    ).astype(jnp.bfloat16)
    mixed = (hidden.astype(jnp.float32) + jax.nn.silu(conv_layer(hidden, w_mid))).astype(
        jnp.bfloat16
    )
    noise_pred = conv_layer(mixed, w_out)
    estimate = (noisy - jnp.sqrt(1.0 - signal_level) * noise_pred) / jnp.sqrt(signal_level)
    depth_full = kdata.shape[2]
    rows_full = sens.shape[3]
    width = sens.shape[4]
    blocks = (
        dft_blocks(rows_full, False),
        dft_blocks(depth_full, False),
        dft_blocks(rows_full, True),
        dft_blocks(depth_full, True),
    )
    kdata_x = along_last(kdata, dft_blocks(width, True))
    weight = mask.astype(jnp.float32)[None, None, :, :, None]

    def operator(image, with_data):
        return combine_coils(
            coil_term(gather_rows(image), sens, kdata_x, weight, blocks, with_data)
        )

    solution = estimate
    residual = operator(estimate, True)
    direction = image = curvature = norm_now = None
    for iteration in range(ITERS):
        final_turn = iteration + 1 == ITERS
        residual_image = operator(residual, False) + REG_WEIGHT * residual
        if direction is None:
            sums = global_sums(
                jnp.stack([jnp.sum(residual * residual), jnp.sum(residual * residual_image)])
            )
            norm_next = sums[0]
            curvature = sums[1]
            direction = residual
            image = residual_image
        else:
            sums = global_sums(
                jnp.stack(
                    [
                        jnp.sum(residual * residual),
                        jnp.sum(residual * residual_image),
                        jnp.sum(residual * image),
                        jnp.sum(direction * residual_image),
                    ]
                )
            )
            norm_next = sums[0]
            ratio = norm_next / norm_now
            curvature = sums[1] + ratio * (sums[2] + sums[3]) + ratio * ratio * curvature
            direction = residual + ratio * direction
            image = residual_image + ratio * image
        norm_now = norm_next
        step_size = norm_now / curvature
        solution = solution + step_size * direction
        if not final_turn:
            residual = residual - step_size * image
    recon = solution
    next_sample = jnp.sqrt(prior_level) * recon + jnp.sqrt(1.0 - prior_level) * noise_pred
    return (recon, next_sample)


def solution(mesh):
    return jax.shard_map(
        body,
        mesh=mesh,
        in_specs=(
            P(None, "slab", "coil", None),
            P(),
            P(),
            P(),
            P(),
            P(),
            P("coil", None, "slab", None, None),
            P("coil", None, None, "slab", None),
            P(None, "slab"),
        ),
        out_specs=(P(None, "slab", "coil", None), P(None, "slab", "coil", None)),
        check_vma=False,
    )
```

```python
import math

import jax
import jax.numpy as jnp
from jax import lax
from jax.sharding import PartitionSpec as P

ITERS = 2
STEPS = 1000
STRIDE = 20


REG_WEIGHT = 0.5
HIGHEST_PRECISION = lax.Precision.HIGHEST


def extended(cells, sides, width):
    for axis, dim in sides:
        count = lax.axis_size(axis)
        ends = count - 1
        head = lax.slice_in_dim(cells, 0, width, axis=dim)
        tail = lax.slice_in_dim(cells, cells.shape[dim] - width, cells.shape[dim], axis=dim)
        cells = jnp.concatenate(
            [
                lax.ppermute(tail, axis, [(i, (i + 1) % count) for i in range(ends)]),
                cells,
                lax.ppermute(head, axis, [((i + 1) % count, i) for i in range(ends)]),
            ],
            axis=dim,
        )
    return cells


def plan_level(step_value):
    angle = (step_value / STEPS + 0.008) / 1.008 * (math.pi / 2)
    return jnp.cos(angle) ** 2


def time_bias(step_value, time_weight):
    half = time_weight.shape[0] // 2
    freqs = jnp.exp(-math.log(10000.0) * jnp.arange(half, dtype=jnp.float32) / half)
    phase = step_value * freqs
    embed = jnp.concatenate([jnp.sin(phase), jnp.cos(phase)])
    return jnp.dot(embed, time_weight, precision=HIGHEST_PRECISION)


def conv_padded(padded, weights):
    depth, rows, width = (padded.shape[1] - 2, padded.shape[2] - 2, padded.shape[3])
    total = jnp.zeros((weights.shape[3], depth, rows, width), jnp.float32)
    for depth_shift in range(3):
        for row_shift in range(3):
            window = padded[:, depth_shift : depth_shift + depth, row_shift : row_shift + rows, :]
            taps = jnp.einsum(
                "aoc,czyx->aozyx",
                weights[depth_shift, row_shift],
                window,
                preferred_element_type=jnp.float32,
            )
            shifted = jnp.pad(taps, ((0, 0), (0, 0), (0, 0), (0, 0), (1, 1)))
            total = (
                total
                + shifted[0, ..., 0:width]
                + shifted[1, ..., 1 : width + 1]
                + shifted[2, ..., 2 : width + 2]
            )
    return total


def conv_layer(inputs, weights):
    return conv_padded(extended(inputs, (("slab", 1), ("coil", 2)), 1), weights)


def conv_columns(padded, weights):
    depth, rows, width = (padded.shape[1] - 2, padded.shape[2] - 2, padded.shape[3])
    wide = jnp.pad(padded, ((0, 0), (0, 0), (0, 0), (1, 1)))
    windows = [
        wide[:, a : a + depth, b : b + rows, c : c + width]
        for a in range(3)
        for b in range(3)
        for c in range(3)
    ]
    columns = jnp.stack(windows, axis=0).reshape((-1, depth, rows, width))
    matrix = jnp.transpose(weights, (3, 0, 1, 2, 4)).reshape((weights.shape[3], -1))
    return jnp.einsum("ok,kzyx->ozyx", matrix, columns, preferred_element_type=jnp.float32)


def inside_volume(depth, rows):
    slab, slabs = lax.axis_index("slab"), lax.axis_size("slab")
    coil, coils = lax.axis_index("coil"), lax.axis_size("coil")
    plane = jnp.arange(depth)
    row = jnp.arange(rows)
    plane_ok = ~(((plane == 0) & (slab == 0)) | ((plane == depth - 1) & (slab == slabs - 1)))
    row_ok = ~(((row == 0) & (coil == 0)) | ((row == rows - 1) & (coil == coils - 1)))
    return plane_ok[:, None, None] & row_ok[None, :, None]


def dft_blocks(length, inverse):
    index = jnp.arange(length, dtype=jnp.int32)
    product = index[:, None] * index[None, :] % length
    theta = product.astype(jnp.float32) * (2.0 * math.pi / length)
    cosine = jnp.cos(theta) / math.sqrt(length)
    sine = jnp.sin(theta) / math.sqrt(length)
    if inverse:
        sine = -sine
    upper = jnp.stack([cosine, sine], axis=1)
    lower = jnp.stack([-sine, cosine], axis=1)
    return jnp.stack([upper, lower], axis=0)


def along_last(data, blocks):
    return jnp.einsum("pkqn,cqzyn->cpzyk", blocks, data, precision=HIGHEST_PRECISION)


def along_rows(data, blocks):
    return jnp.einsum("pkqn,cqzny->cpzky", blocks, data, precision=HIGHEST_PRECISION)


def along_depth(data, blocks):
    return jnp.einsum("pkqn,cqnyx->cpkyx", blocks, data, precision=HIGHEST_PRECISION)


def times_sens(sens, image):
    real_part = sens[:, 0] * image[0] - sens[:, 1] * image[1]
    imag_part = sens[:, 0] * image[1] + sens[:, 1] * image[0]
    return jnp.stack([real_part, imag_part], axis=1)


def times_conj(sens, images):
    real_part = jnp.sum(sens[:, 0] * images[:, 0] + sens[:, 1] * images[:, 1], axis=0)
    imag_part = jnp.sum(sens[:, 0] * images[:, 1] - sens[:, 1] * images[:, 0], axis=0)
    return jnp.stack([real_part, imag_part])


def coil_term(image_full, sens, kdata_x, weight, blocks, with_data):
    forward_y, forward_z, inverse_y, inverse_z = blocks
    coil_images = times_sens(sens, image_full)
    spectrum = along_rows(coil_images, forward_y)
    pencils = lax.all_to_all(
        spectrum.astype(jnp.bfloat16), "slab", split_axis=3, concat_axis=2, tiled=True
    ).astype(jnp.float32)
    kspace = along_depth(pencils, forward_z)
    if with_data:
        kspace = weight * (kdata_x - kspace)
    else:
        kspace = weight * kspace
    back = along_depth(kspace, inverse_z)
    slabs = lax.all_to_all(
        back.astype(jnp.bfloat16), "slab", split_axis=2, concat_axis=3, tiled=True
    ).astype(jnp.float32)
    images = along_rows(slabs, inverse_y)
    return times_conj(sens, images)


def combine_coils(partial_value):
    count = lax.axis_size("coil")
    pieces = lax.all_to_all(partial_value, "coil", split_axis=2, concat_axis=0, tiled=True)
    pieces = pieces.reshape((count, partial_value.shape[0]) + pieces.shape[1:])
    return jnp.sum(pieces, axis=0)


def gather_rows(value):
    return lax.all_gather(value, "coil", axis=2, tiled=True)


def global_sums(values):
    axes = ("slab", "coil")
    count = lax.axis_size("slab") * lax.axis_size("coil")
    spread = jnp.broadcast_to(values[None], (count,) + values.shape)
    return jnp.sum(lax.all_to_all(spread, axes, split_axis=0, concat_axis=0, tiled=True), axis=0)


def body(noisy, step_index, w_in, w_mid, w_out, time_weight, sens, kdata, mask):
    step_value = step_index.astype(jnp.float32)
    signal_level = plan_level(step_value)
    prior_level = plan_level(step_value - STRIDE)
    bias = time_bias(step_value, time_weight)
    noisy_wide = extended(noisy.astype(jnp.bfloat16), (("slab", 1), ("coil", 2)), 2)
    hidden_wide = jax.nn.silu(conv_columns(noisy_wide, w_in) + bias[:, None, None, None])
    hidden_wide = jnp.where(
        inside_volume(hidden_wide.shape[1], hidden_wide.shape[2]), hidden_wide, 0.0
    ).astype(jnp.bfloat16)
    hidden = hidden_wide[:, 1:-1, 1:-1, :]
    mixed = (hidden.astype(jnp.float32) + jax.nn.silu(conv_padded(hidden_wide, w_mid))).astype(
        jnp.bfloat16
    )
    noise_pred = conv_layer(mixed, w_out)
    estimate = (noisy - jnp.sqrt(1.0 - signal_level) * noise_pred) / jnp.sqrt(signal_level)
    depth_full = kdata.shape[2]
    rows_full = sens.shape[3]
    width = sens.shape[4]
    blocks = (
        dft_blocks(rows_full, False),
        dft_blocks(depth_full, False),
        dft_blocks(rows_full, True),
        dft_blocks(depth_full, True),
    )
    kdata_x = along_last(kdata, dft_blocks(width, True))
    weight = mask.astype(jnp.float32)[None, None, :, :, None]

    def operator(image, with_data):
        return combine_coils(
            coil_term(gather_rows(image), sens, kdata_x, weight, blocks, with_data)
        )

    solution = estimate
    residual = operator(estimate, True)
    direction = image = curvature = norm_now = None
    for iteration in range(ITERS):
        final_turn = iteration + 1 == ITERS
        residual_image = operator(residual, False) + REG_WEIGHT * residual
        if direction is None:
            sums = global_sums(
                jnp.stack([jnp.sum(residual * residual), jnp.sum(residual * residual_image)])
            )
            norm_next = sums[0]
            curvature = sums[1]
            direction = residual
            image = residual_image
        else:
            sums = global_sums(
                jnp.stack(
                    [
                        jnp.sum(residual * residual),
                        jnp.sum(residual * residual_image),
                        jnp.sum(residual * image),
                        jnp.sum(direction * residual_image),
                    ]
                )
            )
            norm_next = sums[0]
            ratio = norm_next / norm_now
            curvature = sums[1] + ratio * (sums[2] + sums[3]) + ratio * ratio * curvature
            direction = residual + ratio * direction
            image = residual_image + ratio * image
        norm_now = norm_next
        step_size = norm_now / curvature
        solution = solution + step_size * direction
        if not final_turn:
            residual = residual - step_size * image
    recon = solution
    next_sample = jnp.sqrt(prior_level) * recon + jnp.sqrt(1.0 - prior_level) * noise_pred
    return (recon, next_sample)


def solution(mesh):
    return jax.shard_map(
        body,
        mesh=mesh,
        in_specs=(
            P(None, "slab", "coil", None),
            P(),
            P(),
            P(),
            P(),
            P(),
            P("coil", None, "slab", None, None),
            P("coil", None, None, "slab", None),
            P(None, "slab"),
        ),
        out_specs=(P(None, "slab", "coil", None), P(None, "slab", "coil", None)),
        check_vma=False,
    )
```

```python
import math

import jax
import jax.numpy as jnp
from jax import lax
from jax.sharding import PartitionSpec as P

ITERS = 2
STEPS = 1000
STRIDE = 20


REG_WEIGHT = 0.5
HIGHEST_PRECISION = lax.Precision.HIGHEST


def extended(cells, sides, width):
    for axis, dim in sides:
        count = lax.axis_size(axis)
        ends = count - 1
        head = lax.slice_in_dim(cells, 0, width, axis=dim)
        tail = lax.slice_in_dim(cells, cells.shape[dim] - width, cells.shape[dim], axis=dim)
        cells = jnp.concatenate(
            [
                lax.ppermute(tail, axis, [(i, (i + 1) % count) for i in range(ends)]),
                cells,
                lax.ppermute(head, axis, [((i + 1) % count, i) for i in range(ends)]),
            ],
            axis=dim,
        )
    return cells


def plan_level(step_value):
    angle = (step_value / STEPS + 0.008) / 1.008 * (math.pi / 2)
    return jnp.cos(angle) ** 2


def time_bias(step_value, time_weight):
    half = time_weight.shape[0] // 2
    freqs = jnp.exp(-math.log(10000.0) * jnp.arange(half, dtype=jnp.float32) / half)
    phase = step_value * freqs
    embed = jnp.concatenate([jnp.sin(phase), jnp.cos(phase)])
    return jnp.dot(embed, time_weight, precision=HIGHEST_PRECISION)


def conv_padded(padded, weights):
    depth, rows, width = (padded.shape[1] - 2, padded.shape[2] - 2, padded.shape[3])
    total = jnp.zeros((weights.shape[3], depth, rows, width), jnp.float32)
    for depth_shift in range(3):
        for row_shift in range(3):
            window = padded[:, depth_shift : depth_shift + depth, row_shift : row_shift + rows, :]
            taps = jnp.einsum(
                "aoc,czyx->aozyx",
                weights[depth_shift, row_shift],
                window,
                preferred_element_type=jnp.float32,
            )
            shifted = jnp.pad(taps, ((0, 0), (0, 0), (0, 0), (0, 0), (1, 1)))
            total = (
                total
                + shifted[0, ..., 0:width]
                + shifted[1, ..., 1 : width + 1]
                + shifted[2, ..., 2 : width + 2]
            )
    return total


def conv_layer(inputs, weights):
    return conv_padded(extended(inputs, (("slab", 1), ("coil", 2)), 1), weights)


def conv_columns(padded, weights):
    depth, rows, width = (padded.shape[1] - 2, padded.shape[2] - 2, padded.shape[3])
    wide = jnp.pad(padded, ((0, 0), (0, 0), (0, 0), (1, 1)))
    windows = [
        wide[:, a : a + depth, b : b + rows, c : c + width]
        for a in range(3)
        for b in range(3)
        for c in range(3)
    ]
    columns = jnp.stack(windows, axis=0).reshape((-1, depth, rows, width))
    matrix = jnp.transpose(weights, (3, 0, 1, 2, 4)).reshape((weights.shape[3], -1))
    return jnp.einsum("ok,kzyx->ozyx", matrix, columns, preferred_element_type=jnp.float32)


def inside_volume(depth, rows):
    slab, slabs = lax.axis_index("slab"), lax.axis_size("slab")
    coil, coils = lax.axis_index("coil"), lax.axis_size("coil")
    plane = jnp.arange(depth)
    row = jnp.arange(rows)
    plane_ok = ~(((plane == 0) & (slab == 0)) | ((plane == depth - 1) & (slab == slabs - 1)))
    row_ok = ~(((row == 0) & (coil == 0)) | ((row == rows - 1) & (coil == coils - 1)))
    return plane_ok[:, None, None] & row_ok[None, :, None]


def dft_blocks(length, inverse):
    index = jnp.arange(length, dtype=jnp.int32)
    product = index[:, None] * index[None, :] % length
    theta = product.astype(jnp.float32) * (2.0 * math.pi / length)
    cosine = jnp.cos(theta) / math.sqrt(length)
    sine = jnp.sin(theta) / math.sqrt(length)
    if inverse:
        sine = -sine
    upper = jnp.stack([cosine, sine], axis=1)
    lower = jnp.stack([-sine, cosine], axis=1)
    return jnp.stack([upper, lower], axis=0)


def along_last(data, blocks):
    return jnp.einsum("pkqn,cqzyn->cpzyk", blocks, data, precision=HIGHEST_PRECISION)


def along_rows(data, blocks):
    return jnp.einsum("pkqn,cqzny->cpzky", blocks, data, precision=HIGHEST_PRECISION)


def along_depth(data, blocks):
    return jnp.einsum("pkqn,cqnyx->cpkyx", blocks, data, precision=HIGHEST_PRECISION)


def times_sens(sens, image):
    real_part = sens[:, 0] * image[0] - sens[:, 1] * image[1]
    imag_part = sens[:, 0] * image[1] + sens[:, 1] * image[0]
    return jnp.stack([real_part, imag_part], axis=1)


def times_conj(sens, images):
    real_part = jnp.sum(sens[:, 0] * images[:, 0] + sens[:, 1] * images[:, 1], axis=0)
    imag_part = jnp.sum(sens[:, 0] * images[:, 1] - sens[:, 1] * images[:, 0], axis=0)
    return jnp.stack([real_part, imag_part])


def coil_term(image_full, sens, kdata_x, weight, blocks, with_data):
    forward_y, forward_z, inverse_y, inverse_z = blocks
    coil_images = times_sens(sens, image_full)
    spectrum = along_rows(coil_images, forward_y)
    pencils = lax.all_to_all(
        spectrum.astype(jnp.bfloat16), "slab", split_axis=3, concat_axis=2, tiled=True
    ).astype(jnp.float32)
    kspace = along_depth(pencils, forward_z)
    if with_data:
        kspace = weight * (kdata_x - kspace)
    else:
        kspace = weight * kspace
    back = along_depth(kspace, inverse_z)
    slabs = lax.all_to_all(
        back.astype(jnp.bfloat16), "slab", split_axis=2, concat_axis=3, tiled=True
    ).astype(jnp.float32)
    images = along_rows(slabs, inverse_y)
    return times_conj(sens, images)


def combine_coils(partial_value):
    count = lax.axis_size("coil")
    pieces = lax.all_to_all(partial_value, "coil", split_axis=2, concat_axis=0, tiled=True)
    pieces = pieces.reshape((count, partial_value.shape[0]) + pieces.shape[1:])
    return jnp.sum(pieces, axis=0)


def gather_rows(value):
    return lax.all_gather(value, "coil", axis=2, tiled=True)


def global_sums(values):
    axes = ("slab", "coil")
    count = lax.axis_size("slab") * lax.axis_size("coil")
    spread = jnp.broadcast_to(values[None], (count,) + values.shape)
    return jnp.sum(lax.all_to_all(spread, axes, split_axis=0, concat_axis=0, tiled=True), axis=0)


def body(noisy, step_index, w_in, w_mid, w_out, time_weight, sens, kdata, mask):
    step_value = step_index.astype(jnp.float32)
    signal_level = plan_level(step_value)
    prior_level = plan_level(step_value - STRIDE)
    bias = time_bias(step_value, time_weight)
    noisy_wide = extended(noisy.astype(jnp.bfloat16), (("slab", 1), ("coil", 2)), 2)
    hidden_wide = jax.nn.silu(conv_columns(noisy_wide, w_in) + bias[:, None, None, None])
    hidden_wide = jnp.where(
        inside_volume(hidden_wide.shape[1], hidden_wide.shape[2]), hidden_wide, 0.0
    ).astype(jnp.bfloat16)
    hidden = hidden_wide[:, 1:-1, 1:-1, :]
    mixed = (hidden.astype(jnp.float32) + jax.nn.silu(conv_columns(hidden_wide, w_mid))).astype(
        jnp.bfloat16
    )
    noise_pred = conv_layer(mixed, w_out)
    estimate = (noisy - jnp.sqrt(1.0 - signal_level) * noise_pred) / jnp.sqrt(signal_level)
    depth_full = kdata.shape[2]
    rows_full = sens.shape[3]
    width = sens.shape[4]
    blocks = (
        dft_blocks(rows_full, False),
        dft_blocks(depth_full, False),
        dft_blocks(rows_full, True),
        dft_blocks(depth_full, True),
    )
    kdata_x = along_last(kdata, dft_blocks(width, True))
    weight = mask.astype(jnp.float32)[None, None, :, :, None]

    def operator(image, with_data):
        return combine_coils(
            coil_term(gather_rows(image), sens, kdata_x, weight, blocks, with_data)
        )

    solution = estimate
    residual = operator(estimate, True)
    direction = image = curvature = norm_now = None
    for iteration in range(ITERS):
        final_turn = iteration + 1 == ITERS
        residual_image = operator(residual, False) + REG_WEIGHT * residual
        if direction is None:
            sums = global_sums(
                jnp.stack([jnp.sum(residual * residual), jnp.sum(residual * residual_image)])
            )
            norm_next = sums[0]
            curvature = sums[1]
            direction = residual
            image = residual_image
        else:
            sums = global_sums(
                jnp.stack(
                    [
                        jnp.sum(residual * residual),
                        jnp.sum(residual * residual_image),
                        jnp.sum(residual * image),
                        jnp.sum(direction * residual_image),
                    ]
                )
            )
            norm_next = sums[0]
            ratio = norm_next / norm_now
            curvature = sums[1] + ratio * (sums[2] + sums[3]) + ratio * ratio * curvature
            direction = residual + ratio * direction
            image = residual_image + ratio * image
        norm_now = norm_next
        step_size = norm_now / curvature
        solution = solution + step_size * direction
        if not final_turn:
            residual = residual - step_size * image
    recon = solution
    next_sample = jnp.sqrt(prior_level) * recon + jnp.sqrt(1.0 - prior_level) * noise_pred
    return (recon, next_sample)


def solution(mesh):
    return jax.shard_map(
        body,
        mesh=mesh,
        in_specs=(
            P(None, "slab", "coil", None),
            P(),
            P(),
            P(),
            P(),
            P(),
            P("coil", None, "slab", None, None),
            P("coil", None, None, "slab", None),
            P(None, "slab"),
        ),
        out_specs=(P(None, "slab", "coil", None), P(None, "slab", "coil", None)),
        check_vma=False,
    )
```

```python
import math

import jax
import jax.numpy as jnp
from jax import lax
from jax.sharding import PartitionSpec as P

ITERS = 2
STEPS = 1000
STRIDE = 20


REG_WEIGHT = 0.5
HIGHEST_PRECISION = lax.Precision.HIGHEST


def extended(cells, sides, width):
    for axis, dim in sides:
        count = lax.axis_size(axis)
        ends = count - 1
        head = lax.slice_in_dim(cells, 0, width, axis=dim)
        tail = lax.slice_in_dim(cells, cells.shape[dim] - width, cells.shape[dim], axis=dim)
        cells = jnp.concatenate(
            [
                lax.ppermute(tail, axis, [(i, (i + 1) % count) for i in range(ends)]),
                cells,
                lax.ppermute(head, axis, [((i + 1) % count, i) for i in range(ends)]),
            ],
            axis=dim,
        )
    return cells


def plan_level(step_value):
    angle = (step_value / STEPS + 0.008) / 1.008 * (math.pi / 2)
    return jnp.cos(angle) ** 2


def time_bias(step_value, time_weight):
    half = time_weight.shape[0] // 2
    freqs = jnp.exp(-math.log(10000.0) * jnp.arange(half, dtype=jnp.float32) / half)
    phase = step_value * freqs
    embed = jnp.concatenate([jnp.sin(phase), jnp.cos(phase)])
    return jnp.dot(embed, time_weight, precision=HIGHEST_PRECISION)


def conv_padded(padded, weights):
    depth, rows, width = (padded.shape[1] - 2, padded.shape[2] - 2, padded.shape[3])
    total = jnp.zeros((weights.shape[3], depth, rows, width), jnp.float32)
    for depth_shift in range(3):
        for row_shift in range(3):
            window = padded[:, depth_shift : depth_shift + depth, row_shift : row_shift + rows, :]
            taps = jnp.einsum(
                "aoc,czyx->aozyx",
                weights[depth_shift, row_shift],
                window,
                preferred_element_type=jnp.float32,
            )
            shifted = jnp.pad(taps, ((0, 0), (0, 0), (0, 0), (0, 0), (1, 1)))
            total = (
                total
                + shifted[0, ..., 0:width]
                + shifted[1, ..., 1 : width + 1]
                + shifted[2, ..., 2 : width + 2]
            )
    return total


def conv_layer(inputs, weights):
    return conv_padded(extended(inputs, (("slab", 1), ("coil", 2)), 1), weights)


def conv_columns(padded, weights):
    depth, rows, width = (padded.shape[1] - 2, padded.shape[2] - 2, padded.shape[3])
    wide = jnp.pad(padded, ((0, 0), (0, 0), (0, 0), (1, 1)))
    windows = [
        wide[:, a : a + depth, b : b + rows, c : c + width]
        for a in range(3)
        for b in range(3)
        for c in range(3)
    ]
    columns = jnp.stack(windows, axis=0).reshape((-1, depth, rows, width))
    matrix = jnp.transpose(weights, (3, 0, 1, 2, 4)).reshape((weights.shape[3], -1))
    return jnp.einsum("ok,kzyx->ozyx", matrix, columns, preferred_element_type=jnp.float32)


def inside_volume(depth, rows):
    slab, slabs = lax.axis_index("slab"), lax.axis_size("slab")
    coil, coils = lax.axis_index("coil"), lax.axis_size("coil")
    plane = jnp.arange(depth)
    row = jnp.arange(rows)
    plane_ok = ~(((plane == 0) & (slab == 0)) | ((plane == depth - 1) & (slab == slabs - 1)))
    row_ok = ~(((row == 0) & (coil == 0)) | ((row == rows - 1) & (coil == coils - 1)))
    return plane_ok[:, None, None] & row_ok[None, :, None]


def dft_blocks(length, inverse):
    index = jnp.arange(length, dtype=jnp.int32)
    product = index[:, None] * index[None, :] % length
    theta = product.astype(jnp.float32) * (2.0 * math.pi / length)
    cosine = jnp.cos(theta) / math.sqrt(length)
    sine = jnp.sin(theta) / math.sqrt(length)
    if inverse:
        sine = -sine
    upper = jnp.stack([cosine, sine], axis=1)
    lower = jnp.stack([-sine, cosine], axis=1)
    return jnp.stack([upper, lower], axis=0)


def along_last(data, blocks):
    return jnp.einsum("pkqn,cqzyn->cpzyk", blocks, data, precision=HIGHEST_PRECISION)


def along_rows(data, blocks):
    return jnp.einsum("pkqn,cqzny->cpzky", blocks, data, precision=HIGHEST_PRECISION)


def along_depth(data, blocks):
    return jnp.einsum("pkqn,cqnyx->cpkyx", blocks, data, precision=HIGHEST_PRECISION)


def times_sens(sens, image):
    real_part = sens[:, 0] * image[0] - sens[:, 1] * image[1]
    imag_part = sens[:, 0] * image[1] + sens[:, 1] * image[0]
    return jnp.stack([real_part, imag_part], axis=1)


def times_conj(sens, images):
    real_part = jnp.sum(sens[:, 0] * images[:, 0] + sens[:, 1] * images[:, 1], axis=0)
    imag_part = jnp.sum(sens[:, 0] * images[:, 1] - sens[:, 1] * images[:, 0], axis=0)
    return jnp.stack([real_part, imag_part])


def coil_term(image_full, sens, kdata_x, weight, blocks, with_data):
    forward_y, forward_z, inverse_y, inverse_z = blocks
    coil_images = times_sens(sens, image_full)
    spectrum = along_rows(coil_images, forward_y)
    pencils = lax.all_to_all(
        spectrum.astype(jnp.bfloat16), "slab", split_axis=3, concat_axis=2, tiled=True
    ).astype(jnp.float32)
    kspace = along_depth(pencils, forward_z)
    if with_data:
        kspace = weight * (kdata_x - kspace)
    else:
        kspace = weight * kspace
    back = along_depth(kspace, inverse_z)
    link_type = jnp.float32 if with_data else jnp.bfloat16
    slabs = lax.all_to_all(
        back.astype(link_type), "slab", split_axis=2, concat_axis=3, tiled=True
    ).astype(jnp.float32)
    images = along_rows(slabs, inverse_y)
    return times_conj(sens, images)


def combine_coils(partial_value):
    count = lax.axis_size("coil")
    pieces = lax.all_to_all(partial_value, "coil", split_axis=2, concat_axis=0, tiled=True)
    pieces = pieces.reshape((count, partial_value.shape[0]) + pieces.shape[1:])
    return jnp.sum(pieces, axis=0)


def gather_rows(value):
    return lax.all_gather(value, "coil", axis=2, tiled=True)


def global_sums(values):
    axes = ("slab", "coil")
    count = lax.axis_size("slab") * lax.axis_size("coil")
    spread = jnp.broadcast_to(values[None], (count,) + values.shape)
    return jnp.sum(lax.all_to_all(spread, axes, split_axis=0, concat_axis=0, tiled=True), axis=0)


def body(noisy, step_index, w_in, w_mid, w_out, time_weight, sens, kdata, mask):
    step_value = step_index.astype(jnp.float32)
    signal_level = plan_level(step_value)
    prior_level = plan_level(step_value - STRIDE)
    bias = time_bias(step_value, time_weight)
    noisy_wide = extended(noisy.astype(jnp.bfloat16), (("slab", 1), ("coil", 2)), 2)
    hidden_wide = jax.nn.silu(conv_columns(noisy_wide, w_in) + bias[:, None, None, None])
    hidden_wide = jnp.where(
        inside_volume(hidden_wide.shape[1], hidden_wide.shape[2]), hidden_wide, 0.0
    ).astype(jnp.bfloat16)
    hidden = hidden_wide[:, 1:-1, 1:-1, :]
    mixed = (hidden.astype(jnp.float32) + jax.nn.silu(conv_padded(hidden_wide, w_mid))).astype(
        jnp.bfloat16
    )
    noise_pred = conv_layer(mixed, w_out)
    estimate = (noisy - jnp.sqrt(1.0 - signal_level) * noise_pred) / jnp.sqrt(signal_level)
    depth_full = kdata.shape[2]
    rows_full = sens.shape[3]
    width = sens.shape[4]
    blocks = (
        dft_blocks(rows_full, False),
        dft_blocks(depth_full, False),
        dft_blocks(rows_full, True),
        dft_blocks(depth_full, True),
    )
    kdata_x = along_last(kdata, dft_blocks(width, True))
    weight = mask.astype(jnp.float32)[None, None, :, :, None]

    def operator(image, with_data):
        return combine_coils(
            coil_term(gather_rows(image), sens, kdata_x, weight, blocks, with_data)
        )

    solution = estimate
    residual = operator(estimate, True)
    direction = image = curvature = norm_now = None
    for iteration in range(ITERS):
        final_turn = iteration + 1 == ITERS
        residual_image = operator(residual, False) + REG_WEIGHT * residual
        if direction is None:
            sums = global_sums(
                jnp.stack([jnp.sum(residual * residual), jnp.sum(residual * residual_image)])
            )
            norm_next = sums[0]
            curvature = sums[1]
            direction = residual
            image = residual_image
        else:
            sums = global_sums(
                jnp.stack(
                    [
                        jnp.sum(residual * residual),
                        jnp.sum(residual * residual_image),
                        jnp.sum(residual * image),
                        jnp.sum(direction * residual_image),
                    ]
                )
            )
            norm_next = sums[0]
            ratio = norm_next / norm_now
            curvature = sums[1] + ratio * (sums[2] + sums[3]) + ratio * ratio * curvature
            direction = residual + ratio * direction
            image = residual_image + ratio * image
        norm_now = norm_next
        step_size = norm_now / curvature
        solution = solution + step_size * direction
        if not final_turn:
            residual = residual - step_size * image
    recon = solution
    next_sample = jnp.sqrt(prior_level) * recon + jnp.sqrt(1.0 - prior_level) * noise_pred
    return (recon, next_sample)


def solution(mesh):
    return jax.shard_map(
        body,
        mesh=mesh,
        in_specs=(
            P(None, "slab", "coil", None),
            P(),
            P(),
            P(),
            P(),
            P(),
            P("coil", None, "slab", None, None),
            P("coil", None, None, "slab", None),
            P(None, "slab"),
        ),
        out_specs=(P(None, "slab", "coil", None), P(None, "slab", "coil", None)),
        check_vma=False,
    )
```

```python
import math

import jax
import jax.numpy as jnp
from jax import lax
from jax.sharding import PartitionSpec as P

ITERS = 2
STEPS = 1000
STRIDE = 20


REG_WEIGHT = 0.5
HIGHEST_PRECISION = lax.Precision.HIGHEST
TRANSFORM_PRECISION = lax.Precision.HIGH


def extended(cells, sides, width):
    for axis, dim in sides:
        count = lax.axis_size(axis)
        ends = count - 1
        head = lax.slice_in_dim(cells, 0, width, axis=dim)
        tail = lax.slice_in_dim(cells, cells.shape[dim] - width, cells.shape[dim], axis=dim)
        cells = jnp.concatenate(
            [
                lax.ppermute(tail, axis, [(i, (i + 1) % count) for i in range(ends)]),
                cells,
                lax.ppermute(head, axis, [((i + 1) % count, i) for i in range(ends)]),
            ],
            axis=dim,
        )
    return cells


def plan_level(step_value):
    angle = (step_value / STEPS + 0.008) / 1.008 * (math.pi / 2)
    return jnp.cos(angle) ** 2


def time_bias(step_value, time_weight):
    half = time_weight.shape[0] // 2
    freqs = jnp.exp(-math.log(10000.0) * jnp.arange(half, dtype=jnp.float32) / half)
    phase = step_value * freqs
    embed = jnp.concatenate([jnp.sin(phase), jnp.cos(phase)])
    return jnp.dot(embed, time_weight, precision=HIGHEST_PRECISION)


def conv_padded(padded, weights):
    depth, rows, width = (padded.shape[1] - 2, padded.shape[2] - 2, padded.shape[3])
    total = jnp.zeros((weights.shape[3], depth, rows, width), jnp.float32)
    for depth_shift in range(3):
        for row_shift in range(3):
            window = padded[:, depth_shift : depth_shift + depth, row_shift : row_shift + rows, :]
            taps = jnp.einsum(
                "aoc,czyx->aozyx",
                weights[depth_shift, row_shift],
                window,
                preferred_element_type=jnp.float32,
            )
            shifted = jnp.pad(taps, ((0, 0), (0, 0), (0, 0), (0, 0), (1, 1)))
            total = (
                total
                + shifted[0, ..., 0:width]
                + shifted[1, ..., 1 : width + 1]
                + shifted[2, ..., 2 : width + 2]
            )
    return total


def conv_layer(inputs, weights):
    return conv_padded(extended(inputs, (("slab", 1), ("coil", 2)), 1), weights)


def conv_columns(padded, weights):
    depth, rows, width = (padded.shape[1] - 2, padded.shape[2] - 2, padded.shape[3])
    wide = jnp.pad(padded, ((0, 0), (0, 0), (0, 0), (1, 1)))
    windows = [
        wide[:, a : a + depth, b : b + rows, c : c + width]
        for a in range(3)
        for b in range(3)
        for c in range(3)
    ]
    columns = jnp.stack(windows, axis=0).reshape((-1, depth, rows, width))
    matrix = jnp.transpose(weights, (3, 0, 1, 2, 4)).reshape((weights.shape[3], -1))
    return jnp.einsum("ok,kzyx->ozyx", matrix, columns, preferred_element_type=jnp.float32)


def inside_volume(depth, rows):
    slab, slabs = lax.axis_index("slab"), lax.axis_size("slab")
    coil, coils = lax.axis_index("coil"), lax.axis_size("coil")
    plane = jnp.arange(depth)
    row = jnp.arange(rows)
    plane_ok = ~(((plane == 0) & (slab == 0)) | ((plane == depth - 1) & (slab == slabs - 1)))
    row_ok = ~(((row == 0) & (coil == 0)) | ((row == rows - 1) & (coil == coils - 1)))
    return plane_ok[:, None, None] & row_ok[None, :, None]


def dft_blocks(length, inverse):
    index = jnp.arange(length, dtype=jnp.int32)
    product = index[:, None] * index[None, :] % length
    theta = product.astype(jnp.float32) * (2.0 * math.pi / length)
    cosine = jnp.cos(theta) / math.sqrt(length)
    sine = jnp.sin(theta) / math.sqrt(length)
    if inverse:
        sine = -sine
    upper = jnp.stack([cosine, sine], axis=1)
    lower = jnp.stack([-sine, cosine], axis=1)
    return jnp.stack([upper, lower], axis=0)


def along_last(data, blocks):
    return jnp.einsum("pkqn,cqzyn->cpzyk", blocks, data, precision=TRANSFORM_PRECISION)


def along_rows(data, blocks):
    return jnp.einsum("pkqn,cqzny->cpzky", blocks, data, precision=TRANSFORM_PRECISION)


def along_depth(data, blocks):
    return jnp.einsum("pkqn,cqnyx->cpkyx", blocks, data, precision=TRANSFORM_PRECISION)


def times_sens(sens, image):
    real_part = sens[:, 0] * image[0] - sens[:, 1] * image[1]
    imag_part = sens[:, 0] * image[1] + sens[:, 1] * image[0]
    return jnp.stack([real_part, imag_part], axis=1)


def times_conj(sens, images):
    real_part = jnp.sum(sens[:, 0] * images[:, 0] + sens[:, 1] * images[:, 1], axis=0)
    imag_part = jnp.sum(sens[:, 0] * images[:, 1] - sens[:, 1] * images[:, 0], axis=0)
    return jnp.stack([real_part, imag_part])


def coil_term(image_full, sens, kdata_x, weight, blocks, with_data):
    forward_y, forward_z, inverse_y, inverse_z = blocks
    coil_images = times_sens(sens, image_full)
    spectrum = along_rows(coil_images, forward_y)
    pencils = lax.all_to_all(
        spectrum.astype(jnp.bfloat16), "slab", split_axis=3, concat_axis=2, tiled=True
    ).astype(jnp.float32)
    kspace = along_depth(pencils, forward_z)
    if with_data:
        kspace = weight * (kdata_x - kspace)
    else:
        kspace = weight * kspace
    back = along_depth(kspace, inverse_z)
    link_type = jnp.float32 if with_data else jnp.bfloat16
    slabs = lax.all_to_all(
        back.astype(link_type), "slab", split_axis=2, concat_axis=3, tiled=True
    ).astype(jnp.float32)
    images = along_rows(slabs, inverse_y)
    return times_conj(sens, images)


def combine_coils(partial_value):
    count = lax.axis_size("coil")
    pieces = lax.all_to_all(partial_value, "coil", split_axis=2, concat_axis=0, tiled=True)
    pieces = pieces.reshape((count, partial_value.shape[0]) + pieces.shape[1:])
    return jnp.sum(pieces, axis=0)


def gather_rows(value):
    return lax.all_gather(value, "coil", axis=2, tiled=True)


def global_sums(values):
    axes = ("slab", "coil")
    count = lax.axis_size("slab") * lax.axis_size("coil")
    spread = jnp.broadcast_to(values[None], (count,) + values.shape)
    return jnp.sum(lax.all_to_all(spread, axes, split_axis=0, concat_axis=0, tiled=True), axis=0)


def body(noisy, step_index, w_in, w_mid, w_out, time_weight, sens, kdata, mask):
    step_value = step_index.astype(jnp.float32)
    signal_level = plan_level(step_value)
    prior_level = plan_level(step_value - STRIDE)
    bias = time_bias(step_value, time_weight)
    noisy_wide = extended(noisy.astype(jnp.bfloat16), (("slab", 1), ("coil", 2)), 2)
    hidden_wide = jax.nn.silu(conv_columns(noisy_wide, w_in) + bias[:, None, None, None])
    hidden_wide = jnp.where(
        inside_volume(hidden_wide.shape[1], hidden_wide.shape[2]), hidden_wide, 0.0
    ).astype(jnp.bfloat16)
    hidden = hidden_wide[:, 1:-1, 1:-1, :]
    mixed = (hidden.astype(jnp.float32) + jax.nn.silu(conv_padded(hidden_wide, w_mid))).astype(
        jnp.bfloat16
    )
    noise_pred = conv_layer(mixed, w_out)
    estimate = (noisy - jnp.sqrt(1.0 - signal_level) * noise_pred) / jnp.sqrt(signal_level)
    depth_full = kdata.shape[2]
    rows_full = sens.shape[3]
    width = sens.shape[4]
    blocks = (
        dft_blocks(rows_full, False),
        dft_blocks(depth_full, False),
        dft_blocks(rows_full, True),
        dft_blocks(depth_full, True),
    )
    kdata_x = along_last(kdata, dft_blocks(width, True))
    weight = mask.astype(jnp.float32)[None, None, :, :, None]

    def operator(image, with_data):
        return combine_coils(
            coil_term(gather_rows(image), sens, kdata_x, weight, blocks, with_data)
        )

    solution = estimate
    residual = operator(estimate, True)
    direction = image = curvature = norm_now = None
    for iteration in range(ITERS):
        final_turn = iteration + 1 == ITERS
        residual_image = operator(residual, False) + REG_WEIGHT * residual
        if direction is None:
            sums = global_sums(
                jnp.stack([jnp.sum(residual * residual), jnp.sum(residual * residual_image)])
            )
            norm_next = sums[0]
            curvature = sums[1]
            direction = residual
            image = residual_image
        else:
            sums = global_sums(
                jnp.stack(
                    [
                        jnp.sum(residual * residual),
                        jnp.sum(residual * residual_image),
                        jnp.sum(residual * image),
                        jnp.sum(direction * residual_image),
                    ]
                )
            )
            norm_next = sums[0]
            ratio = norm_next / norm_now
            curvature = sums[1] + ratio * (sums[2] + sums[3]) + ratio * ratio * curvature
            direction = residual + ratio * direction
            image = residual_image + ratio * image
        norm_now = norm_next
        step_size = norm_now / curvature
        solution = solution + step_size * direction
        if not final_turn:
            residual = residual - step_size * image
    recon = solution
    next_sample = jnp.sqrt(prior_level) * recon + jnp.sqrt(1.0 - prior_level) * noise_pred
    return (recon, next_sample)


def solution(mesh):
    return jax.shard_map(
        body,
        mesh=mesh,
        in_specs=(
            P(None, "slab", "coil", None),
            P(),
            P(),
            P(),
            P(),
            P(),
            P("coil", None, "slab", None, None),
            P("coil", None, None, "slab", None),
            P(None, "slab"),
        ),
        out_specs=(P(None, "slab", "coil", None), P(None, "slab", "coil", None)),
        check_vma=False,
    )
```

```python
import math

import jax
import jax.numpy as jnp
from jax import lax
from jax.sharding import PartitionSpec as P

ITERS = 2
STEPS = 1000
STRIDE = 20


REG_WEIGHT = 0.5
HIGHEST_PRECISION = lax.Precision.HIGHEST
TRANSFORM_PRECISION = lax.Precision.HIGH


def extended(cells, sides, width):
    for axis, dim in sides:
        count = lax.axis_size(axis)
        ends = count - 1
        head = lax.slice_in_dim(cells, 0, width, axis=dim)
        tail = lax.slice_in_dim(cells, cells.shape[dim] - width, cells.shape[dim], axis=dim)
        cells = jnp.concatenate(
            [
                lax.ppermute(tail, axis, [(i, (i + 1) % count) for i in range(ends)]),
                cells,
                lax.ppermute(head, axis, [((i + 1) % count, i) for i in range(ends)]),
            ],
            axis=dim,
        )
    return cells


def plan_level(step_value):
    angle = (step_value / STEPS + 0.008) / 1.008 * (math.pi / 2)
    return jnp.cos(angle) ** 2


def time_bias(step_value, time_weight):
    half = time_weight.shape[0] // 2
    freqs = jnp.exp(-math.log(10000.0) * jnp.arange(half, dtype=jnp.float32) / half)
    phase = step_value * freqs
    embed = jnp.concatenate([jnp.sin(phase), jnp.cos(phase)])
    return jnp.dot(embed, time_weight, precision=HIGHEST_PRECISION)


def conv_padded(padded, weights):
    depth, rows, width = (padded.shape[1] - 2, padded.shape[2] - 2, padded.shape[3])
    total = jnp.zeros((weights.shape[3], depth, rows, width), jnp.float32)
    for depth_shift in range(3):
        for row_shift in range(3):
            window = padded[:, depth_shift : depth_shift + depth, row_shift : row_shift + rows, :]
            taps = jnp.einsum(
                "aoc,czyx->aozyx",
                weights[depth_shift, row_shift],
                window,
                preferred_element_type=jnp.float32,
            )
            shifted = jnp.pad(taps, ((0, 0), (0, 0), (0, 0), (0, 0), (1, 1)))
            total = (
                total
                + shifted[0, ..., 0:width]
                + shifted[1, ..., 1 : width + 1]
                + shifted[2, ..., 2 : width + 2]
            )
    return total


def conv_layer(inputs, weights):
    return conv_padded(extended(inputs, (("slab", 1), ("coil", 2)), 1), weights)


def conv_shifted(padded, weights):
    depth, rows, width = (padded.shape[1] - 2, padded.shape[2] - 2, padded.shape[3])
    wide = jnp.pad(padded, ((0, 0), (0, 0), (0, 0), (1, 1)))
    stacked = jnp.concatenate([wide[..., c : c + width] for c in range(3)], axis=0)
    total = jnp.zeros((weights.shape[3], depth, rows, width), jnp.float32)
    for depth_shift in range(3):
        for row_shift in range(3):
            window = stacked[:, depth_shift : depth_shift + depth, row_shift : row_shift + rows, :]
            matrix = jnp.transpose(weights[depth_shift, row_shift], (1, 0, 2))
            matrix = matrix.reshape((weights.shape[3], -1))
            total = total + jnp.einsum(
                "ok,kzyx->ozyx", matrix, window, preferred_element_type=jnp.float32
            )
    return total


def conv_columns(padded, weights):
    depth, rows, width = (padded.shape[1] - 2, padded.shape[2] - 2, padded.shape[3])
    wide = jnp.pad(padded, ((0, 0), (0, 0), (0, 0), (1, 1)))
    windows = [
        wide[:, a : a + depth, b : b + rows, c : c + width]
        for a in range(3)
        for b in range(3)
        for c in range(3)
    ]
    columns = jnp.stack(windows, axis=0).reshape((-1, depth, rows, width))
    matrix = jnp.transpose(weights, (3, 0, 1, 2, 4)).reshape((weights.shape[3], -1))
    return jnp.einsum("ok,kzyx->ozyx", matrix, columns, preferred_element_type=jnp.float32)


def inside_volume(depth, rows):
    slab, slabs = lax.axis_index("slab"), lax.axis_size("slab")
    coil, coils = lax.axis_index("coil"), lax.axis_size("coil")
    plane = jnp.arange(depth)
    row = jnp.arange(rows)
    plane_ok = ~(((plane == 0) & (slab == 0)) | ((plane == depth - 1) & (slab == slabs - 1)))
    row_ok = ~(((row == 0) & (coil == 0)) | ((row == rows - 1) & (coil == coils - 1)))
    return plane_ok[:, None, None] & row_ok[None, :, None]


def dft_blocks(length, inverse):
    index = jnp.arange(length, dtype=jnp.int32)
    product = index[:, None] * index[None, :] % length
    theta = product.astype(jnp.float32) * (2.0 * math.pi / length)
    cosine = jnp.cos(theta) / math.sqrt(length)
    sine = jnp.sin(theta) / math.sqrt(length)
    if inverse:
        sine = -sine
    upper = jnp.stack([cosine, sine], axis=1)
    lower = jnp.stack([-sine, cosine], axis=1)
    return jnp.stack([upper, lower], axis=0)


def along_last(data, blocks):
    return jnp.einsum("pkqn,cqzyn->cpzyk", blocks, data, precision=TRANSFORM_PRECISION)


def along_rows(data, blocks):
    return jnp.einsum("pkqn,cqzny->cpzky", blocks, data, precision=TRANSFORM_PRECISION)


def along_depth(data, blocks):
    return jnp.einsum("pkqn,cqnyx->cpkyx", blocks, data, precision=TRANSFORM_PRECISION)


def times_sens(sens, image):
    real_part = sens[:, 0] * image[0] - sens[:, 1] * image[1]
    imag_part = sens[:, 0] * image[1] + sens[:, 1] * image[0]
    return jnp.stack([real_part, imag_part], axis=1)


def times_conj(sens, images):
    real_part = jnp.sum(sens[:, 0] * images[:, 0] + sens[:, 1] * images[:, 1], axis=0)
    imag_part = jnp.sum(sens[:, 0] * images[:, 1] - sens[:, 1] * images[:, 0], axis=0)
    return jnp.stack([real_part, imag_part])


def coil_term(image_full, sens, kdata_x, weight, blocks, with_data):
    forward_y, forward_z, inverse_y, inverse_z = blocks
    coil_images = times_sens(sens, image_full)
    spectrum = along_rows(coil_images, forward_y)
    pencils = lax.all_to_all(
        spectrum.astype(jnp.bfloat16), "slab", split_axis=3, concat_axis=2, tiled=True
    ).astype(jnp.float32)
    kspace = along_depth(pencils, forward_z)
    if with_data:
        kspace = weight * (kdata_x - kspace)
    else:
        kspace = weight * kspace
    back = along_depth(kspace, inverse_z)
    link_type = jnp.float32 if with_data else jnp.bfloat16
    slabs = lax.all_to_all(
        back.astype(link_type), "slab", split_axis=2, concat_axis=3, tiled=True
    ).astype(jnp.float32)
    images = along_rows(slabs, inverse_y)
    return times_conj(sens, images)


def combine_coils(partial_value):
    count = lax.axis_size("coil")
    pieces = lax.all_to_all(partial_value, "coil", split_axis=2, concat_axis=0, tiled=True)
    pieces = pieces.reshape((count, partial_value.shape[0]) + pieces.shape[1:])
    return jnp.sum(pieces, axis=0)


def gather_rows(value):
    return lax.all_gather(value, "coil", axis=2, tiled=True)


def global_sums(values):
    axes = ("slab", "coil")
    count = lax.axis_size("slab") * lax.axis_size("coil")
    spread = jnp.broadcast_to(values[None], (count,) + values.shape)
    return jnp.sum(lax.all_to_all(spread, axes, split_axis=0, concat_axis=0, tiled=True), axis=0)


def body(noisy, step_index, w_in, w_mid, w_out, time_weight, sens, kdata, mask):
    step_value = step_index.astype(jnp.float32)
    signal_level = plan_level(step_value)
    prior_level = plan_level(step_value - STRIDE)
    bias = time_bias(step_value, time_weight)
    noisy_wide = extended(noisy.astype(jnp.bfloat16), (("slab", 1), ("coil", 2)), 2)
    hidden_wide = jax.nn.silu(conv_columns(noisy_wide, w_in) + bias[:, None, None, None])
    hidden_wide = jnp.where(
        inside_volume(hidden_wide.shape[1], hidden_wide.shape[2]), hidden_wide, 0.0
    ).astype(jnp.bfloat16)
    hidden = hidden_wide[:, 1:-1, 1:-1, :]
    mixed = (hidden.astype(jnp.float32) + jax.nn.silu(conv_shifted(hidden_wide, w_mid))).astype(
        jnp.bfloat16
    )
    noise_pred = conv_layer(mixed, w_out)
    estimate = (noisy - jnp.sqrt(1.0 - signal_level) * noise_pred) / jnp.sqrt(signal_level)
    depth_full = kdata.shape[2]
    rows_full = sens.shape[3]
    width = sens.shape[4]
    blocks = (
        dft_blocks(rows_full, False),
        dft_blocks(depth_full, False),
        dft_blocks(rows_full, True),
        dft_blocks(depth_full, True),
    )
    kdata_x = along_last(kdata, dft_blocks(width, True))
    weight = mask.astype(jnp.float32)[None, None, :, :, None]

    def operator(image, with_data):
        return combine_coils(
            coil_term(gather_rows(image), sens, kdata_x, weight, blocks, with_data)
        )

    solution = estimate
    residual = operator(estimate, True)
    direction = image = curvature = norm_now = None
    for iteration in range(ITERS):
        final_turn = iteration + 1 == ITERS
        residual_image = operator(residual, False) + REG_WEIGHT * residual
        if direction is None:
            sums = global_sums(
                jnp.stack([jnp.sum(residual * residual), jnp.sum(residual * residual_image)])
            )
            norm_next = sums[0]
            curvature = sums[1]
            direction = residual
            image = residual_image
        else:
            sums = global_sums(
                jnp.stack(
                    [
                        jnp.sum(residual * residual),
                        jnp.sum(residual * residual_image),
                        jnp.sum(residual * image),
                        jnp.sum(direction * residual_image),
                    ]
                )
            )
            norm_next = sums[0]
            ratio = norm_next / norm_now
            curvature = sums[1] + ratio * (sums[2] + sums[3]) + ratio * ratio * curvature
            direction = residual + ratio * direction
            image = residual_image + ratio * image
        norm_now = norm_next
        step_size = norm_now / curvature
        solution = solution + step_size * direction
        if not final_turn:
            residual = residual - step_size * image
    recon = solution
    next_sample = jnp.sqrt(prior_level) * recon + jnp.sqrt(1.0 - prior_level) * noise_pred
    return (recon, next_sample)


def solution(mesh):
    return jax.shard_map(
        body,
        mesh=mesh,
        in_specs=(
            P(None, "slab", "coil", None),
            P(),
            P(),
            P(),
            P(),
            P(),
            P("coil", None, "slab", None, None),
            P("coil", None, None, "slab", None),
            P(None, "slab"),
        ),
        out_specs=(P(None, "slab", "coil", None), P(None, "slab", "coil", None)),
        check_vma=False,
    )
```

```python
import math

import jax
import jax.numpy as jnp
from jax import lax
from jax.sharding import PartitionSpec as P

ITERS = 2
STEPS = 1000
STRIDE = 20


REG_WEIGHT = 0.5
HIGHEST_PRECISION = lax.Precision.HIGHEST
TRANSFORM_PRECISION = lax.Precision.HIGH


def extended(cells, sides, width):
    for axis, dim in sides:
        count = lax.axis_size(axis)
        ends = count - 1
        head = lax.slice_in_dim(cells, 0, width, axis=dim)
        tail = lax.slice_in_dim(cells, cells.shape[dim] - width, cells.shape[dim], axis=dim)
        cells = jnp.concatenate(
            [
                lax.ppermute(tail, axis, [(i, (i + 1) % count) for i in range(ends)]),
                cells,
                lax.ppermute(head, axis, [((i + 1) % count, i) for i in range(ends)]),
            ],
            axis=dim,
        )
    return cells


def plan_level(step_value):
    angle = (step_value / STEPS + 0.008) / 1.008 * (math.pi / 2)
    return jnp.cos(angle) ** 2


def time_bias(step_value, time_weight):
    half = time_weight.shape[0] // 2
    freqs = jnp.exp(-math.log(10000.0) * jnp.arange(half, dtype=jnp.float32) / half)
    phase = step_value * freqs
    embed = jnp.concatenate([jnp.sin(phase), jnp.cos(phase)])
    return jnp.dot(embed, time_weight, precision=HIGHEST_PRECISION)


def conv_padded(padded, weights):
    depth, rows, width = (padded.shape[1] - 2, padded.shape[2] - 2, padded.shape[3])
    total = jnp.zeros((weights.shape[3], depth, rows, width), jnp.float32)
    for depth_shift in range(3):
        for row_shift in range(3):
            window = padded[:, depth_shift : depth_shift + depth, row_shift : row_shift + rows, :]
            taps = jnp.einsum(
                "aoc,czyx->aozyx",
                weights[depth_shift, row_shift],
                window,
                preferred_element_type=jnp.float32,
            )
            shifted = jnp.pad(taps, ((0, 0), (0, 0), (0, 0), (0, 0), (1, 1)))
            total = (
                total
                + shifted[0, ..., 0:width]
                + shifted[1, ..., 1 : width + 1]
                + shifted[2, ..., 2 : width + 2]
            )
    return total


def conv_layer(inputs, weights):
    return conv_padded(extended(inputs, (("slab", 1), ("coil", 2)), 1), weights)


def conv_shifted(padded, weights):
    depth, rows, width = (padded.shape[1] - 2, padded.shape[2] - 2, padded.shape[3])
    wide = jnp.pad(padded, ((0, 0), (0, 0), (0, 0), (1, 1)))
    stacked = jnp.concatenate([wide[..., c : c + width] for c in range(3)], axis=0)
    total = jnp.zeros((weights.shape[3], depth, rows, width), jnp.float32)
    for depth_shift in range(3):
        for row_shift in range(3):
            window = stacked[:, depth_shift : depth_shift + depth, row_shift : row_shift + rows, :]
            matrix = jnp.transpose(weights[depth_shift, row_shift], (1, 0, 2))
            matrix = matrix.reshape((weights.shape[3], -1))
            total = total + jnp.einsum(
                "ok,kzyx->ozyx", matrix, window, preferred_element_type=jnp.float32
            )
    return total


def conv_columns(padded, weights):
    depth, rows, width = (padded.shape[1] - 2, padded.shape[2] - 2, padded.shape[3])
    wide = jnp.pad(padded, ((0, 0), (0, 0), (0, 0), (1, 1)))
    windows = [
        wide[:, a : a + depth, b : b + rows, c : c + width]
        for a in range(3)
        for b in range(3)
        for c in range(3)
    ]
    columns = jnp.stack(windows, axis=0).reshape((-1, depth, rows, width))
    matrix = jnp.transpose(weights, (3, 0, 1, 2, 4)).reshape((weights.shape[3], -1))
    return jnp.einsum("ok,kzyx->ozyx", matrix, columns, preferred_element_type=jnp.float32)


def inside_volume(depth, rows, border):
    slab, slabs = lax.axis_index("slab"), lax.axis_size("slab")
    coil, coils = lax.axis_index("coil"), lax.axis_size("coil")
    block_depth, block_rows = depth - 2 * border, rows - 2 * border
    plane = slab * block_depth + jnp.arange(depth) - border
    row = coil * block_rows + jnp.arange(rows) - border
    plane_ok = (plane >= 0) & (plane < slabs * block_depth)
    row_ok = (row >= 0) & (row < coils * block_rows)
    return plane_ok[:, None, None] & row_ok[None, :, None]


def depth_halo(cells, width):
    count = lax.axis_size("slab")
    depth = cells.shape[1]
    near = extended(cells, (("slab", 1),), depth)
    extra = width - depth
    head = lax.slice_in_dim(cells, 0, extra, axis=1)
    tail = lax.slice_in_dim(cells, depth - extra, depth, axis=1)
    below = lax.ppermute(tail, "slab", [(i, i + 2) for i in range(count - 2)])
    above = lax.ppermute(head, "slab", [(i + 2, i) for i in range(count - 2)])
    return jnp.concatenate([below, near, above], axis=1)


def dft_blocks(length, inverse):
    index = jnp.arange(length, dtype=jnp.int32)
    product = index[:, None] * index[None, :] % length
    theta = product.astype(jnp.float32) * (2.0 * math.pi / length)
    cosine = jnp.cos(theta) / math.sqrt(length)
    sine = jnp.sin(theta) / math.sqrt(length)
    if inverse:
        sine = -sine
    upper = jnp.stack([cosine, sine], axis=1)
    lower = jnp.stack([-sine, cosine], axis=1)
    return jnp.stack([upper, lower], axis=0)


def along_last(data, blocks):
    return jnp.einsum("pkqn,cqzyn->cpzyk", blocks, data, precision=TRANSFORM_PRECISION)


def along_rows(data, blocks):
    return jnp.einsum("pkqn,cqzny->cpzky", blocks, data, precision=TRANSFORM_PRECISION)


def along_depth(data, blocks):
    return jnp.einsum("pkqn,cqnyx->cpkyx", blocks, data, precision=TRANSFORM_PRECISION)


def times_sens(sens, image):
    real_part = sens[:, 0] * image[0] - sens[:, 1] * image[1]
    imag_part = sens[:, 0] * image[1] + sens[:, 1] * image[0]
    return jnp.stack([real_part, imag_part], axis=1)


def times_conj(sens, images):
    real_part = jnp.sum(sens[:, 0] * images[:, 0] + sens[:, 1] * images[:, 1], axis=0)
    imag_part = jnp.sum(sens[:, 0] * images[:, 1] - sens[:, 1] * images[:, 0], axis=0)
    return jnp.stack([real_part, imag_part])


def coil_term(image_full, sens, kdata_x, weight, blocks, with_data):
    forward_y, forward_z, inverse_y, inverse_z = blocks
    coil_images = times_sens(sens, image_full)
    spectrum = along_rows(coil_images, forward_y)
    pencils = lax.all_to_all(
        spectrum.astype(jnp.bfloat16), "slab", split_axis=3, concat_axis=2, tiled=True
    ).astype(jnp.float32)
    kspace = along_depth(pencils, forward_z)
    if with_data:
        kspace = weight * (kdata_x - kspace)
    else:
        kspace = weight * kspace
    back = along_depth(kspace, inverse_z)
    link_type = jnp.float32 if with_data else jnp.bfloat16
    slabs = lax.all_to_all(
        back.astype(link_type), "slab", split_axis=2, concat_axis=3, tiled=True
    ).astype(jnp.float32)
    images = along_rows(slabs, inverse_y)
    return times_conj(sens, images)


def combine_coils(partial_value):
    count = lax.axis_size("coil")
    pieces = lax.all_to_all(partial_value, "coil", split_axis=2, concat_axis=0, tiled=True)
    pieces = pieces.reshape((count, partial_value.shape[0]) + pieces.shape[1:])
    return jnp.sum(pieces, axis=0)


def gather_rows(value):
    return lax.all_gather(value, "coil", axis=2, tiled=True)


def global_sums(values):
    axes = ("slab", "coil")
    count = lax.axis_size("slab") * lax.axis_size("coil")
    spread = jnp.broadcast_to(values[None], (count,) + values.shape)
    return jnp.sum(lax.all_to_all(spread, axes, split_axis=0, concat_axis=0, tiled=True), axis=0)


def body(noisy, step_index, w_in, w_mid, w_out, time_weight, sens, kdata, mask):
    step_value = step_index.astype(jnp.float32)
    signal_level = plan_level(step_value)
    prior_level = plan_level(step_value - STRIDE)
    bias = time_bias(step_value, time_weight)
    noisy_deep = depth_halo(noisy.astype(jnp.bfloat16), 3)
    noisy_wide = extended(noisy_deep, (("coil", 2),), 3)
    hidden_wide = jax.nn.silu(conv_columns(noisy_wide, w_in) + bias[:, None, None, None])
    hidden_wide = jnp.where(
        inside_volume(hidden_wide.shape[1], hidden_wide.shape[2], 2), hidden_wide, 0.0
    ).astype(jnp.bfloat16)
    mixed_wide = hidden_wide[:, 1:-1, 1:-1, :].astype(jnp.float32) + jax.nn.silu(
        conv_shifted(hidden_wide, w_mid)
    )
    mixed_wide = jnp.where(
        inside_volume(mixed_wide.shape[1], mixed_wide.shape[2], 1), mixed_wide, 0.0
    ).astype(jnp.bfloat16)
    noise_pred = conv_padded(mixed_wide, w_out)
    estimate = (noisy - jnp.sqrt(1.0 - signal_level) * noise_pred) / jnp.sqrt(signal_level)
    depth_full = kdata.shape[2]
    rows_full = sens.shape[3]
    width = sens.shape[4]
    blocks = (
        dft_blocks(rows_full, False),
        dft_blocks(depth_full, False),
        dft_blocks(rows_full, True),
        dft_blocks(depth_full, True),
    )
    kdata_x = along_last(kdata, dft_blocks(width, True))
    weight = mask.astype(jnp.float32)[None, None, :, :, None]

    def operator(image, with_data):
        return combine_coils(
            coil_term(gather_rows(image), sens, kdata_x, weight, blocks, with_data)
        )

    solution = estimate
    residual = operator(estimate, True)
    direction = image = curvature = norm_now = None
    for iteration in range(ITERS):
        final_turn = iteration + 1 == ITERS
        residual_image = operator(residual, False) + REG_WEIGHT * residual
        if direction is None:
            sums = global_sums(
                jnp.stack([jnp.sum(residual * residual), jnp.sum(residual * residual_image)])
            )
            norm_next = sums[0]
            curvature = sums[1]
            direction = residual
            image = residual_image
        else:
            sums = global_sums(
                jnp.stack(
                    [
                        jnp.sum(residual * residual),
                        jnp.sum(residual * residual_image),
                        jnp.sum(residual * image),
                        jnp.sum(direction * residual_image),
                    ]
                )
            )
            norm_next = sums[0]
            ratio = norm_next / norm_now
            curvature = sums[1] + ratio * (sums[2] + sums[3]) + ratio * ratio * curvature
            direction = residual + ratio * direction
            image = residual_image + ratio * image
        norm_now = norm_next
        step_size = norm_now / curvature
        solution = solution + step_size * direction
        if not final_turn:
            residual = residual - step_size * image
    recon = solution
    next_sample = jnp.sqrt(prior_level) * recon + jnp.sqrt(1.0 - prior_level) * noise_pred
    return (recon, next_sample)


def solution(mesh):
    return jax.shard_map(
        body,
        mesh=mesh,
        in_specs=(
            P(None, "slab", "coil", None),
            P(),
            P(),
            P(),
            P(),
            P(),
            P("coil", None, "slab", None, None),
            P("coil", None, None, "slab", None),
            P(None, "slab"),
        ),
        out_specs=(P(None, "slab", "coil", None), P(None, "slab", "coil", None)),
        check_vma=False,
    )
```

```python
import math

import jax
import jax.numpy as jnp
from jax import lax
from jax.sharding import PartitionSpec as P

ITERS = 2
STEPS = 1000
STRIDE = 20


REG_WEIGHT = 0.5
HIGHEST_PRECISION = lax.Precision.HIGHEST
TRANSFORM_PRECISION = lax.Precision.HIGH


def extended(cells, sides, width):
    for axis, dim in sides:
        count = lax.axis_size(axis)
        ends = count - 1
        head = lax.slice_in_dim(cells, 0, width, axis=dim)
        tail = lax.slice_in_dim(cells, cells.shape[dim] - width, cells.shape[dim], axis=dim)
        cells = jnp.concatenate(
            [
                lax.ppermute(tail, axis, [(i, (i + 1) % count) for i in range(ends)]),
                cells,
                lax.ppermute(head, axis, [((i + 1) % count, i) for i in range(ends)]),
            ],
            axis=dim,
        )
    return cells


def plan_level(step_value):
    angle = (step_value / STEPS + 0.008) / 1.008 * (math.pi / 2)
    return jnp.cos(angle) ** 2


def time_bias(step_value, time_weight):
    half = time_weight.shape[0] // 2
    freqs = jnp.exp(-math.log(10000.0) * jnp.arange(half, dtype=jnp.float32) / half)
    phase = step_value * freqs
    embed = jnp.concatenate([jnp.sin(phase), jnp.cos(phase)])
    return jnp.dot(embed, time_weight, precision=HIGHEST_PRECISION)


def conv_padded(padded, weights):
    depth, rows, width = (padded.shape[1] - 2, padded.shape[2] - 2, padded.shape[3])
    total = jnp.zeros((weights.shape[3], depth, rows, width), jnp.float32)
    for depth_shift in range(3):
        for row_shift in range(3):
            window = padded[:, depth_shift : depth_shift + depth, row_shift : row_shift + rows, :]
            taps = jnp.einsum(
                "aoc,czyx->aozyx",
                weights[depth_shift, row_shift],
                window,
                preferred_element_type=jnp.float32,
            )
            shifted = jnp.pad(taps, ((0, 0), (0, 0), (0, 0), (0, 0), (1, 1)))
            total = (
                total
                + shifted[0, ..., 0:width]
                + shifted[1, ..., 1 : width + 1]
                + shifted[2, ..., 2 : width + 2]
            )
    return total


def conv_layer(inputs, weights):
    return conv_padded(extended(inputs, (("slab", 1), ("coil", 2)), 1), weights)


def conv_shifted(padded, weights):
    depth, rows, width = (padded.shape[1] - 2, padded.shape[2] - 2, padded.shape[3])
    wide = jnp.pad(padded, ((0, 0), (0, 0), (0, 0), (1, 1)))
    stacked = jnp.concatenate([wide[..., c : c + width] for c in range(3)], axis=0)
    total = jnp.zeros((weights.shape[3], depth, rows, width), jnp.float32)
    for depth_shift in range(3):
        for row_shift in range(3):
            window = stacked[:, depth_shift : depth_shift + depth, row_shift : row_shift + rows, :]
            matrix = jnp.transpose(weights[depth_shift, row_shift], (1, 0, 2))
            matrix = matrix.reshape((weights.shape[3], -1))
            total = total + jnp.einsum(
                "ok,kzyx->ozyx", matrix, window, preferred_element_type=jnp.float32
            )
    return total


def conv_columns(padded, weights):
    depth, rows, width = (padded.shape[1] - 2, padded.shape[2] - 2, padded.shape[3])
    wide = jnp.pad(padded, ((0, 0), (0, 0), (0, 0), (1, 1)))
    windows = [
        wide[:, a : a + depth, b : b + rows, c : c + width]
        for a in range(3)
        for b in range(3)
        for c in range(3)
    ]
    columns = jnp.stack(windows, axis=0).reshape((-1, depth, rows, width))
    matrix = jnp.transpose(weights, (3, 0, 1, 2, 4)).reshape((weights.shape[3], -1))
    return jnp.einsum("ok,kzyx->ozyx", matrix, columns, preferred_element_type=jnp.float32)


def inside_volume(depth, rows):
    slab, slabs = lax.axis_index("slab"), lax.axis_size("slab")
    coil, coils = lax.axis_index("coil"), lax.axis_size("coil")
    plane = jnp.arange(depth)
    row = jnp.arange(rows)
    plane_ok = ~(((plane == 0) & (slab == 0)) | ((plane == depth - 1) & (slab == slabs - 1)))
    row_ok = ~(((row == 0) & (coil == 0)) | ((row == rows - 1) & (coil == coils - 1)))
    return plane_ok[:, None, None] & row_ok[None, :, None]


def dft_blocks(length, inverse):
    index = jnp.arange(length, dtype=jnp.int32)
    product = index[:, None] * index[None, :] % length
    theta = product.astype(jnp.float32) * (2.0 * math.pi / length)
    cosine = jnp.cos(theta) / math.sqrt(length)
    sine = jnp.sin(theta) / math.sqrt(length)
    if inverse:
        sine = -sine
    upper = jnp.stack([cosine, sine], axis=1)
    lower = jnp.stack([-sine, cosine], axis=1)
    return jnp.stack([upper, lower], axis=0)


def along_last(data, blocks):
    return jnp.einsum("pkqn,cqzyn->cpzyk", blocks, data, precision=TRANSFORM_PRECISION)


def along_rows(data, blocks):
    return jnp.einsum("pkqn,cqzny->cpzky", blocks, data, precision=TRANSFORM_PRECISION)


def along_depth(data, blocks):
    return jnp.einsum("pkqn,cqnyx->cpkyx", blocks, data, precision=TRANSFORM_PRECISION)


def times_sens(sens, image):
    real_part = sens[:, 0] * image[0] - sens[:, 1] * image[1]
    imag_part = sens[:, 0] * image[1] + sens[:, 1] * image[0]
    return jnp.stack([real_part, imag_part], axis=1)


def times_conj(sens, images):
    real_part = jnp.sum(sens[:, 0] * images[:, 0] + sens[:, 1] * images[:, 1], axis=0)
    imag_part = jnp.sum(sens[:, 0] * images[:, 1] - sens[:, 1] * images[:, 0], axis=0)
    return jnp.stack([real_part, imag_part])


def coil_term(image_full, sens, kdata_x, weight, blocks, with_data):
    forward_y, forward_z, inverse_y, inverse_z = blocks
    coil_images = times_sens(sens, image_full)
    spectrum = along_rows(coil_images, forward_y)
    pencils = lax.all_to_all(
        spectrum.astype(jnp.bfloat16), "slab", split_axis=3, concat_axis=2, tiled=True
    ).astype(jnp.float32)
    kspace = along_depth(pencils, forward_z)
    if with_data:
        kspace = weight * (kdata_x - kspace)
    else:
        kspace = weight * kspace
    back = along_depth(kspace, inverse_z)
    link_type = jnp.float32 if with_data else jnp.bfloat16
    slabs = lax.all_to_all(
        back.astype(link_type), "slab", split_axis=2, concat_axis=3, tiled=True
    ).astype(jnp.float32)
    images = along_rows(slabs, inverse_y)
    return times_conj(sens, images)


def combine_coils(partial_value):
    count = lax.axis_size("coil")
    pieces = lax.all_to_all(partial_value, "coil", split_axis=2, concat_axis=0, tiled=True)
    pieces = pieces.reshape((count, partial_value.shape[0]) + pieces.shape[1:])
    return jnp.sum(pieces, axis=0)


def gather_rows(value):
    return lax.all_gather(value, "coil", axis=2, tiled=True)


def global_sums(values):
    axes = ("slab", "coil")
    count = lax.axis_size("slab") * lax.axis_size("coil")
    spread = jnp.broadcast_to(values[None], (count,) + values.shape)
    return jnp.sum(lax.all_to_all(spread, axes, split_axis=0, concat_axis=0, tiled=True), axis=0)


def body(noisy, step_index, w_in, w_mid, w_out, time_weight, sens, kdata, mask):
    step_value = step_index.astype(jnp.float32)
    signal_level = plan_level(step_value)
    prior_level = plan_level(step_value - STRIDE)
    bias = time_bias(step_value, time_weight)
    noisy_wide = extended(noisy.astype(jnp.bfloat16), (("slab", 1), ("coil", 2)), 2)
    hidden_wide = jax.nn.silu(conv_columns(noisy_wide, w_in) + bias[:, None, None, None])
    hidden_wide = jnp.where(
        inside_volume(hidden_wide.shape[1], hidden_wide.shape[2]), hidden_wide, 0.0
    ).astype(jnp.bfloat16)
    hidden = hidden_wide[:, 1:-1, 1:-1, :]
    mixed = (hidden.astype(jnp.float32) + jax.nn.silu(conv_shifted(hidden_wide, w_mid))).astype(
        jnp.bfloat16
    )
    noise_pred = conv_layer(mixed, w_out)
    estimate = (noisy - jnp.sqrt(1.0 - signal_level) * noise_pred) / jnp.sqrt(signal_level)
    depth_full = kdata.shape[2]
    rows_full = sens.shape[3]
    width = sens.shape[4]
    blocks = (
        dft_blocks(rows_full, False),
        dft_blocks(depth_full, False),
        dft_blocks(rows_full, True),
        dft_blocks(depth_full, True),
    )
    kdata_x = along_last(kdata, dft_blocks(width, True))
    weight = mask.astype(jnp.float32)[None, None, :, :, None]

    def operator(image, with_data):
        return combine_coils(
            coil_term(gather_rows(image), sens, kdata_x, weight, blocks, with_data)
        )

    residual = operator(estimate, True)
    zero = jnp.zeros_like(residual)
    unknown = jnp.full((), jnp.inf, jnp.float32)

    def turn(_, state):
        solution, residual, direction, image, curvature, norm_now = state
        residual_image = operator(residual, False) + REG_WEIGHT * residual
        sums = global_sums(
            jnp.stack(
                [
                    jnp.sum(residual * residual),
                    jnp.sum(residual * residual_image),
                    jnp.sum(residual * image),
                    jnp.sum(direction * residual_image),
                ]
            )
        )
        norm_next = sums[0]
        ratio = norm_next / norm_now
        curvature = sums[1] + ratio * (sums[2] + sums[3]) + ratio * ratio * curvature
        direction = residual + ratio * direction
        image = residual_image + ratio * image
        step_size = norm_next / curvature
        solution = solution + step_size * direction
        residual = residual - step_size * image
        return (solution, residual, direction, image, curvature, norm_next)

    state = (estimate, residual, zero, zero, jnp.zeros((), jnp.float32), unknown)
    solution = lax.fori_loop(0, ITERS, turn, state)[0]
    recon = solution
    next_sample = jnp.sqrt(prior_level) * recon + jnp.sqrt(1.0 - prior_level) * noise_pred
    return (recon, next_sample)


def solution(mesh):
    return jax.shard_map(
        body,
        mesh=mesh,
        in_specs=(
            P(None, "slab", "coil", None),
            P(),
            P(),
            P(),
            P(),
            P(),
            P("coil", None, "slab", None, None),
            P("coil", None, None, "slab", None),
            P(None, "slab"),
        ),
        out_specs=(P(None, "slab", "coil", None), P(None, "slab", "coil", None)),
        check_vma=False,
    )
```

```python
import math

import jax
import jax.numpy as jnp
from jax import lax
from jax.sharding import PartitionSpec as P

ITERS = 2
STEPS = 1000
STRIDE = 20


REG_WEIGHT = 0.5
HIGHEST_PRECISION = lax.Precision.HIGHEST
TRANSFORM_PRECISION = lax.Precision.HIGH


def extended(cells, sides, width):
    for axis, dim in sides:
        count = lax.axis_size(axis)
        ends = count - 1
        head = lax.slice_in_dim(cells, 0, width, axis=dim)
        tail = lax.slice_in_dim(cells, cells.shape[dim] - width, cells.shape[dim], axis=dim)
        cells = jnp.concatenate(
            [
                lax.ppermute(tail, axis, [(i, (i + 1) % count) for i in range(ends)]),
                cells,
                lax.ppermute(head, axis, [((i + 1) % count, i) for i in range(ends)]),
            ],
            axis=dim,
        )
    return cells


def plan_level(step_value):
    angle = (step_value / STEPS + 0.008) / 1.008 * (math.pi / 2)
    return jnp.cos(angle) ** 2


def time_bias(step_value, time_weight):
    half = time_weight.shape[0] // 2
    freqs = jnp.exp(-math.log(10000.0) * jnp.arange(half, dtype=jnp.float32) / half)
    phase = step_value * freqs
    embed = jnp.concatenate([jnp.sin(phase), jnp.cos(phase)])
    return jnp.dot(embed, time_weight, precision=HIGHEST_PRECISION)


def conv_padded(padded, weights):
    depth, rows, width = (padded.shape[1] - 2, padded.shape[2] - 2, padded.shape[3])

    def plane_taps(depth_shift, total):
        planes = lax.dynamic_slice_in_dim(padded, depth_shift, depth, axis=1)
        for row_shift in range(3):
            window = planes[:, :, row_shift : row_shift + rows, :]
            taps = jnp.einsum(
                "aoc,czyx->aozyx",
                weights[depth_shift, row_shift],
                window,
                preferred_element_type=jnp.float32,
            )
            shifted = jnp.pad(taps, ((0, 0), (0, 0), (0, 0), (0, 0), (1, 1)))
            total = (
                total
                + shifted[0, ..., 0:width]
                + shifted[1, ..., 1 : width + 1]
                + shifted[2, ..., 2 : width + 2]
            )
        return total

    total = jnp.zeros((weights.shape[3], depth, rows, width), jnp.float32)
    return lax.fori_loop(0, 3, plane_taps, total)


def conv_layer(inputs, weights):
    return conv_padded(extended(inputs, (("slab", 1), ("coil", 2)), 1), weights)


def conv_shifted(padded, weights):
    depth, rows, width = (padded.shape[1] - 2, padded.shape[2] - 2, padded.shape[3])
    wide = jnp.pad(padded, ((0, 0), (0, 0), (0, 0), (1, 1)))
    stacked = jnp.concatenate([wide[..., c : c + width] for c in range(3)], axis=0)
    def plane_taps(depth_shift, total):
        planes = lax.dynamic_slice_in_dim(stacked, depth_shift, depth, axis=1)
        for row_shift in range(3):
            window = planes[:, :, row_shift : row_shift + rows, :]
            matrix = jnp.transpose(weights[depth_shift, row_shift], (1, 0, 2))
            matrix = matrix.reshape((weights.shape[3], -1))
            total = total + jnp.einsum(
                "ok,kzyx->ozyx", matrix, window, preferred_element_type=jnp.float32
            )
        return total

    total = jnp.zeros((weights.shape[3], depth, rows, width), jnp.float32)
    return lax.fori_loop(0, 3, plane_taps, total)


def conv_columns(padded, weights):
    depth, rows, width = (padded.shape[1] - 2, padded.shape[2] - 2, padded.shape[3])
    wide = jnp.pad(padded, ((0, 0), (0, 0), (0, 0), (1, 1)))
    windows = [
        wide[:, a : a + depth, b : b + rows, c : c + width]
        for a in range(3)
        for b in range(3)
        for c in range(3)
    ]
    columns = jnp.stack(windows, axis=0).reshape((-1, depth, rows, width))
    matrix = jnp.transpose(weights, (3, 0, 1, 2, 4)).reshape((weights.shape[3], -1))
    return jnp.einsum("ok,kzyx->ozyx", matrix, columns, preferred_element_type=jnp.float32)


def inside_volume(depth, rows):
    slab, slabs = lax.axis_index("slab"), lax.axis_size("slab")
    coil, coils = lax.axis_index("coil"), lax.axis_size("coil")
    plane = jnp.arange(depth)
    row = jnp.arange(rows)
    plane_ok = ~(((plane == 0) & (slab == 0)) | ((plane == depth - 1) & (slab == slabs - 1)))
    row_ok = ~(((row == 0) & (coil == 0)) | ((row == rows - 1) & (coil == coils - 1)))
    return plane_ok[:, None, None] & row_ok[None, :, None]


def dft_blocks(length, inverse):
    index = jnp.arange(length, dtype=jnp.int32)
    product = index[:, None] * index[None, :] % length
    theta = product.astype(jnp.float32) * (2.0 * math.pi / length)
    cosine = jnp.cos(theta) / math.sqrt(length)
    sine = jnp.sin(theta) / math.sqrt(length)
    if inverse:
        sine = -sine
    upper = jnp.stack([cosine, sine], axis=1)
    lower = jnp.stack([-sine, cosine], axis=1)
    return jnp.stack([upper, lower], axis=0)


def along_last(data, blocks):
    return jnp.einsum("pkqn,cqzyn->cpzyk", blocks, data, precision=TRANSFORM_PRECISION)


def along_rows(data, blocks):
    return jnp.einsum("pkqn,cqzny->cpzky", blocks, data, precision=TRANSFORM_PRECISION)


def along_depth(data, blocks):
    return jnp.einsum("pkqn,cqnyx->cpkyx", blocks, data, precision=TRANSFORM_PRECISION)


def times_sens(sens, image):
    real_part = sens[:, 0] * image[0] - sens[:, 1] * image[1]
    imag_part = sens[:, 0] * image[1] + sens[:, 1] * image[0]
    return jnp.stack([real_part, imag_part], axis=1)


def times_conj(sens, images):
    real_part = jnp.sum(sens[:, 0] * images[:, 0] + sens[:, 1] * images[:, 1], axis=0)
    imag_part = jnp.sum(sens[:, 0] * images[:, 1] - sens[:, 1] * images[:, 0], axis=0)
    return jnp.stack([real_part, imag_part])


def coil_term(image_full, sens, kdata_x, weight, blocks, with_data):
    forward_y, forward_z, inverse_y, inverse_z = blocks
    coil_images = times_sens(sens, image_full)
    spectrum = along_rows(coil_images, forward_y)
    pencils = lax.all_to_all(
        spectrum.astype(jnp.bfloat16), "slab", split_axis=3, concat_axis=2, tiled=True
    ).astype(jnp.float32)
    kspace = along_depth(pencils, forward_z)
    if with_data:
        kspace = weight * (kdata_x - kspace)
    else:
        kspace = weight * kspace
    back = along_depth(kspace, inverse_z)
    link_type = jnp.float32 if with_data else jnp.bfloat16
    slabs = lax.all_to_all(
        back.astype(link_type), "slab", split_axis=2, concat_axis=3, tiled=True
    ).astype(jnp.float32)
    images = along_rows(slabs, inverse_y)
    return times_conj(sens, images)


def combine_coils(partial_value):
    count = lax.axis_size("coil")
    pieces = lax.all_to_all(partial_value, "coil", split_axis=2, concat_axis=0, tiled=True)
    pieces = pieces.reshape((count, partial_value.shape[0]) + pieces.shape[1:])
    return jnp.sum(pieces, axis=0)


def gather_rows(value):
    return lax.all_gather(value, "coil", axis=2, tiled=True)


def global_sums(values):
    axes = ("slab", "coil")
    count = lax.axis_size("slab") * lax.axis_size("coil")
    spread = jnp.broadcast_to(values[None], (count,) + values.shape)
    return jnp.sum(lax.all_to_all(spread, axes, split_axis=0, concat_axis=0, tiled=True), axis=0)


def body(noisy, step_index, w_in, w_mid, w_out, time_weight, sens, kdata, mask):
    step_value = step_index.astype(jnp.float32)
    signal_level = plan_level(step_value)
    prior_level = plan_level(step_value - STRIDE)
    bias = time_bias(step_value, time_weight)
    noisy_wide = extended(noisy.astype(jnp.bfloat16), (("slab", 1), ("coil", 2)), 2)
    hidden_wide = jax.nn.silu(conv_columns(noisy_wide, w_in) + bias[:, None, None, None])
    hidden_wide = jnp.where(
        inside_volume(hidden_wide.shape[1], hidden_wide.shape[2]), hidden_wide, 0.0
    ).astype(jnp.bfloat16)
    hidden = hidden_wide[:, 1:-1, 1:-1, :]
    mixed = (hidden.astype(jnp.float32) + jax.nn.silu(conv_shifted(hidden_wide, w_mid))).astype(
        jnp.bfloat16
    )
    noise_pred = conv_layer(mixed, w_out)
    estimate = (noisy - jnp.sqrt(1.0 - signal_level) * noise_pred) / jnp.sqrt(signal_level)
    depth_full = kdata.shape[2]
    rows_full = sens.shape[3]
    width = sens.shape[4]
    blocks = (
        dft_blocks(rows_full, False),
        dft_blocks(depth_full, False),
        dft_blocks(rows_full, True),
        dft_blocks(depth_full, True),
    )
    kdata_x = along_last(kdata, dft_blocks(width, True))
    weight = mask.astype(jnp.float32)[None, None, :, :, None]

    def operator(image, with_data):
        return combine_coils(
            coil_term(gather_rows(image), sens, kdata_x, weight, blocks, with_data)
        )

    residual = operator(estimate, True)
    zero = jnp.zeros_like(residual)
    unknown = jnp.full((), jnp.inf, jnp.float32)

    def turn(_, state):
        solution, residual, direction, image, curvature, norm_now = state
        residual_image = operator(residual, False) + REG_WEIGHT * residual
        sums = global_sums(
            jnp.stack(
                [
                    jnp.sum(residual * residual),
                    jnp.sum(residual * residual_image),
                    jnp.sum(residual * image),
                    jnp.sum(direction * residual_image),
                ]
            )
        )
        norm_next = sums[0]
        ratio = norm_next / norm_now
        curvature = sums[1] + ratio * (sums[2] + sums[3]) + ratio * ratio * curvature
        direction = residual + ratio * direction
        image = residual_image + ratio * image
        step_size = norm_next / curvature
        solution = solution + step_size * direction
        residual = residual - step_size * image
        return (solution, residual, direction, image, curvature, norm_next)

    state = (estimate, residual, zero, zero, jnp.zeros((), jnp.float32), unknown)
    solution = lax.fori_loop(0, ITERS, turn, state)[0]
    recon = solution
    next_sample = jnp.sqrt(prior_level) * recon + jnp.sqrt(1.0 - prior_level) * noise_pred
    return (recon, next_sample)


def solution(mesh):
    return jax.shard_map(
        body,
        mesh=mesh,
        in_specs=(
            P(None, "slab", "coil", None),
            P(),
            P(),
            P(),
            P(),
            P(),
            P("coil", None, "slab", None, None),
            P("coil", None, None, "slab", None),
            P(None, "slab"),
        ),
        out_specs=(P(None, "slab", "coil", None), P(None, "slab", "coil", None)),
        check_vma=False,
    )
```

```python
import math

import jax
import jax.numpy as jnp
from jax import lax
from jax.sharding import PartitionSpec as P

ITERS = 2
STEPS = 1000
STRIDE = 20


REG_WEIGHT = 0.5
HIGHEST_PRECISION = lax.Precision.HIGHEST
TRANSFORM_PRECISION = lax.Precision.HIGH


def extended(cells, sides, width):
    for axis, dim in sides:
        count = lax.axis_size(axis)
        ends = count - 1
        head = lax.slice_in_dim(cells, 0, width, axis=dim)
        tail = lax.slice_in_dim(cells, cells.shape[dim] - width, cells.shape[dim], axis=dim)
        cells = jnp.concatenate(
            [
                lax.ppermute(tail, axis, [(i, (i + 1) % count) for i in range(ends)]),
                cells,
                lax.ppermute(head, axis, [((i + 1) % count, i) for i in range(ends)]),
            ],
            axis=dim,
        )
    return cells


def plan_level(step_value):
    angle = (step_value / STEPS + 0.008) / 1.008 * (math.pi / 2)
    return jnp.cos(angle) ** 2


def time_bias(step_value, time_weight):
    half = time_weight.shape[0] // 2
    freqs = jnp.exp(-math.log(10000.0) * jnp.arange(half, dtype=jnp.float32) / half)
    phase = step_value * freqs
    embed = jnp.concatenate([jnp.sin(phase), jnp.cos(phase)])
    return jnp.dot(embed, time_weight, precision=HIGHEST_PRECISION)


def conv_padded(padded, weights):
    depth, rows, width = (padded.shape[1] - 2, padded.shape[2] - 2, padded.shape[3])
    total = jnp.zeros((weights.shape[3], depth, rows, width), jnp.float32)
    for depth_shift in range(3):
        for row_shift in range(3):
            window = padded[:, depth_shift : depth_shift + depth, row_shift : row_shift + rows, :]
            taps = jnp.einsum(
                "aoc,czyx->aozyx",
                weights[depth_shift, row_shift],
                window,
                preferred_element_type=jnp.float32,
            )
            shifted = jnp.pad(taps, ((0, 0), (0, 0), (0, 0), (0, 0), (1, 1)))
            total = (
                total
                + shifted[0, ..., 0:width]
                + shifted[1, ..., 1 : width + 1]
                + shifted[2, ..., 2 : width + 2]
            )
    return total


def conv_layer(inputs, weights):
    return conv_padded(extended(inputs, (("slab", 1), ("coil", 2)), 1), weights)


def conv_shifted(padded, weights):
    depth, rows, width = (padded.shape[1] - 2, padded.shape[2] - 2, padded.shape[3])
    wide = jnp.pad(padded, ((0, 0), (0, 0), (0, 0), (1, 1)))
    stacked = jnp.concatenate([wide[..., c : c + width] for c in range(3)], axis=0)
    total = jnp.zeros((weights.shape[3], depth, rows, width), jnp.float32)
    for depth_shift in range(3):
        for row_shift in range(3):
            window = stacked[:, depth_shift : depth_shift + depth, row_shift : row_shift + rows, :]
            matrix = jnp.transpose(weights[depth_shift, row_shift], (1, 0, 2))
            matrix = matrix.reshape((weights.shape[3], -1))
            total = total + jnp.einsum(
                "ok,kzyx->ozyx", matrix, window, preferred_element_type=jnp.float32
            )
    return total


def conv_columns(padded, weights):
    depth, rows, width = (padded.shape[1] - 2, padded.shape[2] - 2, padded.shape[3])
    wide = jnp.pad(padded, ((0, 0), (0, 0), (0, 0), (1, 1)))
    windows = [
        wide[:, a : a + depth, b : b + rows, c : c + width]
        for a in range(3)
        for b in range(3)
        for c in range(3)
    ]
    columns = jnp.stack(windows, axis=0).reshape((-1, depth, rows, width))
    matrix = jnp.transpose(weights, (3, 0, 1, 2, 4)).reshape((weights.shape[3], -1))
    return jnp.einsum("ok,kzyx->ozyx", matrix, columns, preferred_element_type=jnp.float32)


def inside_volume(depth, rows):
    slab, slabs = lax.axis_index("slab"), lax.axis_size("slab")
    coil, coils = lax.axis_index("coil"), lax.axis_size("coil")
    plane = jnp.arange(depth)
    row = jnp.arange(rows)
    plane_ok = ~(((plane == 0) & (slab == 0)) | ((plane == depth - 1) & (slab == slabs - 1)))
    row_ok = ~(((row == 0) & (coil == 0)) | ((row == rows - 1) & (coil == coils - 1)))
    return plane_ok[:, None, None] & row_ok[None, :, None]


def dft_blocks(length, inverse):
    index = jnp.arange(length, dtype=jnp.int32)
    product = index[:, None] * index[None, :] % length
    theta = product.astype(jnp.float32) * (2.0 * math.pi / length)
    cosine = jnp.cos(theta) / math.sqrt(length)
    sine = jnp.sin(theta) / math.sqrt(length)
    if inverse:
        sine = -sine
    upper = jnp.stack([cosine, sine], axis=1)
    lower = jnp.stack([-sine, cosine], axis=1)
    return jnp.stack([upper, lower], axis=0)


def along_last(data, blocks):
    return jnp.einsum("pkqn,cqzyn->cpzyk", blocks, data, precision=TRANSFORM_PRECISION)


def along_rows(data, blocks):
    return jnp.einsum("pkqn,cqzny->cpzky", blocks, data, precision=TRANSFORM_PRECISION)


def along_depth(data, blocks):
    return jnp.einsum("pkqn,cqnyx->cpkyx", blocks, data, precision=TRANSFORM_PRECISION)


def times_sens(sens, image):
    real_part = sens[:, 0] * image[0] - sens[:, 1] * image[1]
    imag_part = sens[:, 0] * image[1] + sens[:, 1] * image[0]
    return jnp.stack([real_part, imag_part], axis=1)


def times_conj(sens, images):
    real_part = jnp.sum(sens[:, 0] * images[:, 0] + sens[:, 1] * images[:, 1], axis=0)
    imag_part = jnp.sum(sens[:, 0] * images[:, 1] - sens[:, 1] * images[:, 0], axis=0)
    return jnp.stack([real_part, imag_part])


def coil_term(image_full, sens, kdata_x, weight, blocks, with_data):
    forward_y, forward_z, inverse_y, inverse_z = blocks
    coil_images = times_sens(sens, image_full)
    spectrum = along_rows(coil_images, forward_y)
    pencils = lax.all_to_all(
        spectrum.astype(jnp.bfloat16), "slab", split_axis=3, concat_axis=2, tiled=True
    ).astype(jnp.float32)
    kspace = along_depth(pencils, forward_z)
    if with_data:
        kspace = weight * (kdata_x - kspace)
    else:
        kspace = weight * kspace
    back = along_depth(kspace, inverse_z)
    link_type = jnp.float32 if with_data else jnp.bfloat16
    slabs = lax.all_to_all(
        back.astype(link_type), "slab", split_axis=2, concat_axis=3, tiled=True
    ).astype(jnp.float32)
    images = along_rows(slabs, inverse_y)
    return times_conj(sens, images)


def combine_coils(partial_value):
    count = lax.axis_size("coil")
    pieces = lax.all_to_all(partial_value, "coil", split_axis=2, concat_axis=0, tiled=True)
    pieces = pieces.reshape((count, partial_value.shape[0]) + pieces.shape[1:])
    return jnp.sum(pieces, axis=0)


def gather_rows(value):
    return lax.all_gather(value, "coil", axis=2, tiled=True)


def global_sums(values):
    axes = ("slab", "coil")
    count = lax.axis_size("slab") * lax.axis_size("coil")
    spread = jnp.broadcast_to(values[None], (count,) + values.shape)
    return jnp.sum(lax.all_to_all(spread, axes, split_axis=0, concat_axis=0, tiled=True), axis=0)


def body(noisy, step_index, w_in, w_mid, w_out, time_weight, sens, kdata, mask):
    step_value = step_index.astype(jnp.float32)
    signal_level = plan_level(step_value)
    prior_level = plan_level(step_value - STRIDE)
    bias = time_bias(step_value, time_weight)
    noisy_wide = extended(noisy.astype(jnp.bfloat16), (("slab", 1), ("coil", 2)), 2)
    hidden_wide = jax.nn.silu(conv_columns(noisy_wide, w_in) + bias[:, None, None, None])
    hidden_wide = jnp.where(
        inside_volume(hidden_wide.shape[1], hidden_wide.shape[2]), hidden_wide, 0.0
    ).astype(jnp.bfloat16)
    hidden = hidden_wide[:, 1:-1, 1:-1, :]
    mixed = (hidden.astype(jnp.float32) + jax.nn.silu(conv_shifted(hidden_wide, w_mid))).astype(
        jnp.bfloat16
    )
    noise_pred = conv_shifted(extended(mixed, (("slab", 1), ("coil", 2)), 1), w_out)
    estimate = (noisy - jnp.sqrt(1.0 - signal_level) * noise_pred) / jnp.sqrt(signal_level)
    depth_full = kdata.shape[2]
    rows_full = sens.shape[3]
    width = sens.shape[4]
    blocks = (
        dft_blocks(rows_full, False),
        dft_blocks(depth_full, False),
        dft_blocks(rows_full, True),
        dft_blocks(depth_full, True),
    )
    kdata_x = along_last(kdata, dft_blocks(width, True))
    weight = mask.astype(jnp.float32)[None, None, :, :, None]

    def operator(image, with_data):
        return combine_coils(
            coil_term(gather_rows(image), sens, kdata_x, weight, blocks, with_data)
        )

    residual = operator(estimate, True)
    zero = jnp.zeros_like(residual)
    unknown = jnp.full((), jnp.inf, jnp.float32)

    def turn(_, state):
        solution, residual, direction, image, curvature, norm_now = state
        residual_image = operator(residual, False) + REG_WEIGHT * residual
        sums = global_sums(
            jnp.stack(
                [
                    jnp.sum(residual * residual),
                    jnp.sum(residual * residual_image),
                    jnp.sum(residual * image),
                    jnp.sum(direction * residual_image),
                ]
            )
        )
        norm_next = sums[0]
        ratio = norm_next / norm_now
        curvature = sums[1] + ratio * (sums[2] + sums[3]) + ratio * ratio * curvature
        direction = residual + ratio * direction
        image = residual_image + ratio * image
        step_size = norm_next / curvature
        solution = solution + step_size * direction
        residual = residual - step_size * image
        return (solution, residual, direction, image, curvature, norm_next)

    state = (estimate, residual, zero, zero, jnp.zeros((), jnp.float32), unknown)
    solution = lax.fori_loop(0, ITERS, turn, state)[0]
    recon = solution
    next_sample = jnp.sqrt(prior_level) * recon + jnp.sqrt(1.0 - prior_level) * noise_pred
    return (recon, next_sample)


def solution(mesh):
    return jax.shard_map(
        body,
        mesh=mesh,
        in_specs=(
            P(None, "slab", "coil", None),
            P(),
            P(),
            P(),
            P(),
            P(),
            P("coil", None, "slab", None, None),
            P("coil", None, None, "slab", None),
            P(None, "slab"),
        ),
        out_specs=(P(None, "slab", "coil", None), P(None, "slab", "coil", None)),
        check_vma=False,
    )
```
